512 devices in a mesh: rows: 128 (over z, y, core), cols: 4 (over x).
Axes of the slice: x: 4, y: 4, z: 16, core: 2. Of those that a mesh axis runs over, the one named last changes fastest.
Arguments:
- features: bfloat16 [256, 16384], P('cols', 'rows'), may hold values from -6 to 6
- weight_matrix: bfloat16 [256, 256], replicated, may hold values from -0.375 to 0.375
- bias_vector: float32 [256], replicated, may hold values from -3 to 3
- adjacency_tiles: bfloat16 [128, 65, 128, 128], P('rows')
- tile_cols: int32 [128, 65], P('rows'), may hold values from 0 to 127, as said below
- tile_count: int32 [128], P('rows'), may hold values from 25 to 65, as said below
- out_grad: bfloat16 [256, 16384], P('cols', 'rows'), may hold values from -6 to 6
Outputs:
- layer_out: bfloat16 [256, 16384], P('cols', 'rows')
- feature_grad: bfloat16 [256, 16384], P('cols', 'rows')
- weight_grad: float32 [256, 256], P('cols')
- bias_grad: float32 [256], P('cols')
The draws below stay inside these ranges and needn't reach their ends.
Inputs may be any that keep to these rules, and one draw needn't show every extreme that they name: `tile_cols`: the live slots of a row block name distinct column blocks, its own among them; the pattern is symmetric: c is live in row block b exactly when b is live in row block c, and that tile is the transpose of the one of b in c's list. Slots past tile_count hold the row block's own index. Outside the hub's row, every live column block other than the hub lies within 16 blocks of the row block around the cycle of 128 blocks; the hub's own row also holds such band blocks. `tile_count`: exactly one row block, the hub, has all 65 slots live.
All inputs are finite; a program needn't handle non-finite values.
Results may differ from the reference program's by a relative error of at most 0.008.
Values may be sent and summed in bfloat16 or wider, within the bound.
No kernel may reach another device: no remote copies, remote signals or barrier semaphores. Data moves between devices by JAX's collectives and lax.ppermute only.
A program may use at most 64 MiB of HBM per device.

```python
import math
import jax
import jax.numpy as jnp
from jax import lax

F = 256
BLK = 128
NB = 128
NEAR = 12
BAND = 16
HUBS = 20
TPR = 65
NODES = 16384


def tile_pattern(key):
    base_key = jax.random.fold_in(key, 11)
    near_offsets = (jax.random.permutation(jax.random.fold_in(base_key, 1), BAND)[:NEAR] + 1).astype(jnp.int32)
    candidate = jax.random.permutation(jax.random.fold_in(base_key, 3), NB - 2 * BAND - 2)[:2 * HUBS - 1].astype(jnp.int32) + BAND + 1
    candidate = jnp.where(candidate >= NB // 2, candidate + 1, candidate).astype(jnp.int32)
    far_dists = jnp.concatenate([jnp.full((1,), NB // 2, jnp.int32), candidate]).astype(jnp.int32)
    hub_block = jax.random.randint(jax.random.fold_in(base_key, 2), (), 0, NB).astype(jnp.int32)
    block_index = jnp.arange(NB, dtype=jnp.int32)
    base_cols = jnp.concatenate([block_index[:, None], (block_index[:, None] + near_offsets[None, :]) % NB, (block_index[:, None] - near_offsets[None, :] + NB) % NB], axis=1)
    hub_cols = (hub_block + far_dists) % NB
    distance = (block_index - hub_block + NB) % NB
    partner = jnp.any(distance[:, None] == far_dists[None, :], axis=1)
    is_hub = block_index == hub_block
    first_extra = jnp.where(is_hub, hub_cols[0], jnp.where(partner, hub_block, block_index))
    extra_cols = jnp.where(is_hub[:, None], hub_cols[None, :], jnp.broadcast_to(block_index[:, None], (NB, 2 * HUBS)))
    extra_cols = extra_cols.at[:, 0].set(first_extra)
    column_ids = jnp.concatenate([base_cols, extra_cols], axis=1).astype(jnp.int32)
    live_count = 2 * NEAR + 1 + jnp.where(is_hub, 2 * HUBS, partner.astype(jnp.int32))
    return (column_ids, live_count.astype(jnp.int32))


def draw_tile_cols(key, part):
    return tile_pattern(key)[0]


def draw_tile_count(key, part):
    return tile_pattern(key)[1]


def draw_adjacency_tiles(key, part):
    column_ids, live_count = tile_pattern(key)
    row_blocks = jnp.broadcast_to(jnp.arange(NB, dtype=jnp.int32)[:, None], (NB, TPR))
    slot_index = jnp.broadcast_to(jnp.arange(TPR, dtype=jnp.int32)[None, :], (NB, TPR))
    pair_low = jnp.minimum(row_blocks, column_ids)
    pair_high = jnp.maximum(row_blocks, column_ids)
    alive = slot_index < live_count[:, None]
    pair_number = jnp.where(alive, pair_low * NB + pair_high, NB * NB + row_blocks * TPR + slot_index)
    value_key = jax.random.fold_in(key, 23)
    sigma = (BLK * (2 * NEAR + 1)) ** (-0.5)

    def draw_pair(number):
        pair_rng = jax.random.fold_in(value_key, number)
        return jax.random.normal(pair_rng, (BLK, BLK), jnp.float32)
    matrices = jax.vmap(draw_pair)(pair_number.reshape(-1)).reshape(NB, TPR, BLK, BLK)
    swapped = jnp.swapaxes(matrices, 2, 3)
    symmetric = (matrices + swapped) * 0.5 ** 0.5
    diagonal = (row_blocks == column_ids)[:, :, None, None]
    flipped = (row_blocks > column_ids)[:, :, None, None]
    values = jnp.where(diagonal, symmetric, jnp.where(flipped, swapped, matrices)) * sigma
    return values.astype(jnp.bfloat16)


def block_scale(own_key, shape, cuts, smallest, top_value):
    def one(position, blocks):
        draws = jax.random.uniform(jax.random.fold_in(jax.random.fold_in(own_key, 6), position), (blocks,), jnp.float32, smallest / len(cuts), top_value / len(cuts))
        return jnp.repeat(jnp.exp(draws), shape[position] // blocks).reshape((-1,) + (1,) * (len(shape) - position - 1))

    gain = one(*cuts[0])
    for cut in cuts[1:]:
        gain = gain * one(*cut)
    return gain


def scatter_about(rng, shape, deviation, most, pieces=(), held_as=jnp.bfloat16):
    drawn = deviation * jax.random.normal(rng, shape, jnp.float32)
    if pieces:
        drawn = drawn * block_scale(rng, shape, pieces, -0.22, 0.18)
    return jnp.clip(drawn, -most, most).astype(held_as)


def setup_inputs(seed: int = 0) -> dict:
    seeds = jax.random.split(jax.random.key(seed), 8)
    features = scatter_about(seeds[0], (F, NODES), 1.0, 6.0, ((0, 4), (1, 128)))
    weight_matrix = scatter_about(seeds[1], (F, F), F ** -0.5, 0.375)
    bias_vector = scatter_about(seeds[2], (F,), 0.5, 3.0, (), jnp.float32)
    adjacency_tiles = draw_adjacency_tiles(jax.random.fold_in(seeds[7], 71), 0)
    tile_cols = draw_tile_cols(jax.random.fold_in(seeds[7], 71), 0)
    tile_count = draw_tile_count(jax.random.fold_in(seeds[7], 71), 0)
    out_grad = scatter_about(seeds[6], (F, NODES), 1.0, 6.0, ((0, 4), (1, 128)))
    return dict(features=features, weight_matrix=weight_matrix, bias_vector=bias_vector, adjacency_tiles=adjacency_tiles, tile_cols=tile_cols, tile_count=tile_count, out_grad=out_grad)


def reference(features, weight_matrix, bias_vector, adjacency_tiles, tile_cols, tile_count, out_grad):
    block_view = features.reshape(F, NB, BLK)
    slot_index = jnp.arange(TPR, dtype=jnp.int32)
    alive_mask = slot_index[None, :] < tile_count[:, None]

    def forward_block(inputs):
        tile_set, column_ids, alive = inputs
        panel = jnp.take(block_view, column_ids, axis=1).astype(jnp.float32)
        panel = panel * alive[None, :, None].astype(jnp.float32)
        return jnp.einsum('fsk,srk->fr', panel, tile_set.astype(jnp.float32))
    aggregated = lax.map(forward_block, (adjacency_tiles, tile_cols, alive_mask))
    aggregated = aggregated.transpose(1, 0, 2).reshape(F, NODES).astype(jnp.bfloat16)
    preact = jnp.dot(weight_matrix, aggregated, preferred_element_type=jnp.float32) + bias_vector[:, None]
    sigmoid_pre = jax.nn.sigmoid(preact)
    layer_out = (preact * sigmoid_pre).astype(jnp.bfloat16)
    pre_grad = (out_grad.astype(jnp.float32) * sigmoid_pre * (1.0 + preact * (1.0 - sigmoid_pre))).astype(jnp.bfloat16)
    grad_scale = 1.0 / math.sqrt(NODES)
    weight_grad = jnp.dot(pre_grad, aggregated.T, preferred_element_type=jnp.float32) * grad_scale
    bias_grad = lax.optimization_barrier(jnp.sum(pre_grad.astype(jnp.float32), axis=1)) * grad_scale
    agg_grad = jnp.dot(weight_matrix.T, pre_grad, preferred_element_type=jnp.float32).astype(jnp.bfloat16)
    grad_blocks = agg_grad.reshape(F, NB, BLK).transpose(1, 0, 2)

    def adjoint_step(running, inputs):
        tile_set, column_ids, alive, own_block = inputs
        contrib = jnp.einsum('fr,srk->sfk', own_block.astype(jnp.float32), tile_set.astype(jnp.float32))
        contrib = contrib * alive[:, None, None].astype(jnp.float32)
        return (running.at[column_ids].add(contrib), None)
    running = jnp.zeros((NB, F, BLK), jnp.float32)
    running = lax.scan(adjoint_step, running, (adjacency_tiles, tile_cols, alive_mask, grad_blocks))[0]
    feature_grad = running.transpose(1, 0, 2).reshape(F, NODES).astype(jnp.bfloat16)
    return (layer_out, feature_grad, weight_grad, bias_grad)
```

```python
import math

import jax
import jax.numpy as jnp
from jax import lax
from jax.sharding import PartitionSpec as P

BAND = 16


def shifted(x, axis, size, d):
    return lax.ppermute(x, axis, [((i + d) % size, i) for i in range(size)])


def doubling_sum(x, axis, size):
    step = 1
    while step < size:
        x = x + lax.ppermute(x, axis, [(i, i ^ step) for i in range(size)])
        step *= 2
    return x


def band_table(x, size):
    panels = [shifted(x, "rows", size, o) if o else x for o in range(-BAND, BAND + 1)]
    return jnp.stack(panels)


def band_products(table, tiles, index, mask):
    picked = jnp.take(table, index, axis=0)
    picked = jnp.where(mask[:, None, None], picked, jnp.zeros((), picked.dtype))
    return jnp.einsum("sfk,srk->fr", picked, tiles, preferred_element_type=jnp.float32)


def per_device(
    features, weight_matrix, bias_vector, adjacency_tiles, tile_cols, tile_count, out_grad
):
    feature_width, rows_here = features.shape
    rows_count = lax.axis_size("rows")
    cols_count = lax.axis_size("cols")
    assert adjacency_tiles.shape[0] == 1
    assert rows_count & (rows_count - 1) == 0
    row = lax.axis_index("rows")
    col = lax.axis_index("cols")
    tiles = adjacency_tiles[0]
    column_ids = tile_cols[0]
    count = tile_count[0]
    slot_count = column_ids.shape[0]

    alive = jnp.arange(slot_count, dtype=jnp.int32) < count
    offset = (column_ids - row + rows_count // 2) % rows_count - rows_count // 2
    near = jnp.abs(offset) <= BAND
    is_hub = count == slot_count
    near_mask = alive & near
    far = alive & jnp.logical_not(near) & jnp.logical_not(is_hub)
    has_far = jnp.any(far)
    index = jnp.where(near, offset + BAND, BAND)
    far_slot = jnp.argmax(far)
    far_tile = lax.dynamic_index_in_dim(tiles, far_slot, 0, keepdims=False)
    far_tile = jnp.where(has_far, far_tile, jnp.zeros((), far_tile.dtype))

    def hub_terms(x):
        own = jnp.where(is_hub, x, jnp.zeros((), x.dtype)).astype(jnp.float32)
        back = jnp.einsum("fk,kr->fr", x, far_tile, preferred_element_type=jnp.float32)
        return own, back

    def finish(table, hub_panel, hub_sum):
        total = band_products(table, tiles, index, near_mask)
        total = total + jnp.einsum(
            "fk,rk->fr", hub_panel, far_tile, preferred_element_type=jnp.float32
        )
        return total + jnp.where(is_hub, hub_sum, jnp.zeros((), hub_sum.dtype))

    own, back = hub_terms(features)
    reduced = doubling_sum(jnp.concatenate([own, back], axis=1), "rows", rows_count)
    table = band_table(features, rows_count)
    hub_panel = reduced[:, :rows_here].astype(jnp.bfloat16)
    aggregated = finish(table, hub_panel, reduced[:, rows_here:]).astype(jnp.bfloat16)

    def cols_stack(x):
        return jnp.concatenate(
            [x] + [shifted(x, "cols", cols_count, e) for e in range(1, cols_count)], axis=0
        )

    grad_full = cols_stack(out_grad)
    agg_full = cols_stack(aggregated)
    shift = col * feature_width
    weight_rel = jnp.roll(jnp.roll(weight_matrix, -shift, axis=0), -shift, axis=1)
    bias_rel = jnp.roll(bias_vector, -shift)
    preact = (
        jnp.dot(weight_rel, agg_full, preferred_element_type=jnp.float32) + bias_rel[:, None]
    )
    sigmoid_pre = jax.nn.sigmoid(preact)
    layer_out = (preact[:feature_width] * sigmoid_pre[:feature_width]).astype(jnp.bfloat16)
    pre_grad = (
        grad_full.astype(jnp.float32) * sigmoid_pre * (1.0 + preact * (1.0 - sigmoid_pre))
    ).astype(jnp.bfloat16)
    agg_grad = jnp.einsum(
        "oi,on->in", weight_rel[:, :feature_width], pre_grad, preferred_element_type=jnp.float32
    ).astype(jnp.bfloat16)
    own_grad = pre_grad[:feature_width]
    weight_part = jnp.einsum(
        "fn,in->fi", own_grad, agg_full, preferred_element_type=jnp.float32
    )
    weight_part = jnp.roll(weight_part, shift, axis=1)
    bias_part = jnp.sum(own_grad.astype(jnp.float32), axis=1)

    own2, back2 = hub_terms(agg_grad)
    width = weight_part.shape[1]
    bias_block = jnp.broadcast_to(bias_part[:, None], (feature_width, 128))
    packed = jnp.concatenate([own2, back2, weight_part, bias_block], axis=1)
    reduced2 = doubling_sum(packed, "rows", rows_count)
    table2 = band_table(agg_grad, rows_count)
    hub_panel2 = reduced2[:, :rows_here].astype(jnp.bfloat16)
    hub_sum2 = reduced2[:, rows_here : 2 * rows_here]
    feature_grad = finish(table2, hub_panel2, hub_sum2).astype(jnp.bfloat16)
    grad_scale = 1.0 / math.sqrt(rows_here * rows_count)
    weight_grad = reduced2[:, 2 * rows_here : 2 * rows_here + width] * grad_scale
    bias_grad = reduced2[:, 2 * rows_here + width] * grad_scale
    return (layer_out, feature_grad, weight_grad, bias_grad)


def solution(mesh):
    return jax.shard_map(
        per_device,
        mesh=mesh,
        in_specs=(
            P("cols", "rows"),
            P(),
            P(),
            P("rows", None, None, None),
            P("rows", None),
            P("rows"),
            P("cols", "rows"),
        ),
        out_specs=(P("cols", "rows"), P("cols", "rows"), P("cols", None), P("cols")),
        check_vma=False,
    )
```

```python
import math

import jax
import jax.numpy as jnp
from jax import lax
from jax.sharding import PartitionSpec as P

BAND = 16
GROUP_ROUNDS = 4


def shifted(x, axis, size, d):
    return lax.ppermute(x, axis, [((i + d) % size, i) for i in range(size)])


def pair_join(mine, got, upper):
    return jnp.where(upper, jnp.concatenate([got, mine]), jnp.concatenate([mine, got]))


def exchange(panel, acc, row, size):
    lanes = panel.shape[-1]
    block = panel[None]
    for k in range(size.bit_length() - 1):
        step = 1 << k
        upper = (row // step) % 2 == 1
        pairs = [(i, i ^ step) for i in range(size)]
        if k < GROUP_ROUNDS:
            flat = block.reshape(-1, lanes).astype(jnp.float32)
            got = lax.ppermute(jnp.concatenate([flat, acc]), "rows", pairs)
            got_block = got[: flat.shape[0]].reshape(block.shape).astype(block.dtype)
            block = pair_join(block, got_block, upper)
            got_acc = got[flat.shape[0] :]
        else:
            got_acc = lax.ppermute(acc, "rows", pairs)
        acc = acc + got_acc
    group = 1 << GROUP_ROUNDS
    lower = shifted(block, "rows", size, -group)
    higher = shifted(block, "rows", size, group)
    return jnp.concatenate([lower, block, higher]), acc


def band_products(table, tiles, index, mask):
    picked = jnp.take(table, index, axis=0)
    picked = jnp.where(mask[:, None, None], picked, jnp.zeros((), picked.dtype))
    return jnp.einsum("sfk,srk->fr", picked, tiles, preferred_element_type=jnp.float32)


def per_device(
    features, weight_matrix, bias_vector, adjacency_tiles, tile_cols, tile_count, out_grad
):
    feature_width, rows_here = features.shape
    rows_count = lax.axis_size("rows")
    cols_count = lax.axis_size("cols")
    assert adjacency_tiles.shape[0] == 1
    assert rows_count & (rows_count - 1) == 0 and rows_count >= 4 << GROUP_ROUNDS
    assert cols_count & (cols_count - 1) == 0
    row = lax.axis_index("rows")
    col = lax.axis_index("cols")
    tiles = adjacency_tiles[0]
    column_ids = tile_cols[0]
    count = tile_count[0]
    slot_count = column_ids.shape[0]
    group = 1 << GROUP_ROUNDS

    alive = jnp.arange(slot_count, dtype=jnp.int32) < count
    offset = (column_ids - row + rows_count // 2) % rows_count - rows_count // 2
    near = jnp.abs(offset) <= BAND
    is_hub = count == slot_count
    near_mask = alive & near
    far = alive & jnp.logical_not(near) & jnp.logical_not(is_hub)
    has_far = jnp.any(far)
    index = jnp.where(near, offset + row % group + group, group)
    far_slot = jnp.argmax(far)
    far_tile = lax.dynamic_index_in_dim(tiles, far_slot, 0, keepdims=False)
    far_tile = jnp.where(has_far, far_tile, jnp.zeros((), far_tile.dtype))

    def hub_terms(x):
        own = jnp.where(is_hub, x, jnp.zeros((), x.dtype)).astype(jnp.float32)
        back = jnp.einsum("fk,kr->fr", x, far_tile, preferred_element_type=jnp.float32)
        return own, back

    def finish(table, hub_panel, hub_sum):
        total = band_products(table, tiles, index, near_mask)
        total = total + jnp.einsum(
            "fk,rk->fr", hub_panel, far_tile, preferred_element_type=jnp.float32
        )
        return total + jnp.where(is_hub, hub_sum, jnp.zeros((), hub_sum.dtype))

    own, back = hub_terms(features)
    table, reduced = exchange(features, jnp.concatenate([own, back]), row, rows_count)
    hub_panel = reduced[:feature_width].astype(jnp.bfloat16)
    aggregated = finish(table, hub_panel, reduced[feature_width:]).astype(jnp.bfloat16)

    both = jnp.stack([aggregated, out_grad])
    step = 1
    while step < cols_count:
        got = lax.ppermute(both, "cols", [(i, i ^ step) for i in range(cols_count)])
        upper = (col // step) % 2 == 1
        both = jnp.where(
            upper, jnp.concatenate([got, both], axis=1), jnp.concatenate([both, got], axis=1)
        )
        step *= 2
    agg_full = both[0].reshape(-1, rows_here)
    grad_full = both[1].reshape(-1, rows_here)

    preact = (
        jnp.dot(weight_matrix, agg_full, preferred_element_type=jnp.float32)
        + bias_vector[:, None]
    )
    sigmoid_pre = jax.nn.sigmoid(preact)
    pre_grad = (
        grad_full.astype(jnp.float32) * sigmoid_pre * (1.0 + preact * (1.0 - sigmoid_pre))
    ).astype(jnp.bfloat16)
    start = col * feature_width
    own_pre = lax.dynamic_slice_in_dim(preact, start, feature_width, 0)
    own_sig = lax.dynamic_slice_in_dim(sigmoid_pre, start, feature_width, 0)
    layer_out = (own_pre * own_sig).astype(jnp.bfloat16)
    own_grad = lax.dynamic_slice_in_dim(pre_grad, start, feature_width, 0)
    weight_cols = lax.dynamic_slice_in_dim(weight_matrix, start, feature_width, 1)
    agg_grad = jnp.einsum(
        "oi,on->in", weight_cols, pre_grad, preferred_element_type=jnp.float32
    ).astype(jnp.bfloat16)
    weight_part = jnp.einsum(
        "fn,in->fi", own_grad, agg_full, preferred_element_type=jnp.float32
    )
    bias_part = jnp.sum(own_grad.astype(jnp.float32), axis=1)

    own2, back2 = hub_terms(agg_grad)
    width = weight_part.shape[1]
    lanes = rows_here
    bias_rows = jnp.zeros((8, lanes), jnp.float32).at[0, :feature_width].set(bias_part)
    packed = jnp.concatenate(
        [own2, back2, weight_part.reshape(-1, lanes), bias_rows]
    )
    table2, reduced2 = exchange(agg_grad, packed, row, rows_count)
    hub_panel2 = reduced2[:feature_width].astype(jnp.bfloat16)
    hub_sum2 = reduced2[feature_width : 2 * feature_width]
    feature_grad = finish(table2, hub_panel2, hub_sum2).astype(jnp.bfloat16)
    grad_scale = 1.0 / math.sqrt(rows_here * rows_count)
    weight_rows = feature_width * width // lanes
    weight_grad = (
        reduced2[2 * feature_width : 2 * feature_width + weight_rows].reshape(feature_width, width)
        * grad_scale
    )
    bias_grad = reduced2[2 * feature_width + weight_rows, :feature_width] * grad_scale
    return (layer_out, feature_grad, weight_grad, bias_grad)


def solution(mesh):
    return jax.shard_map(
        per_device,
        mesh=mesh,
        in_specs=(
            P("cols", "rows"),
            P(),
            P(),
            P("rows", None, None, None),
            P("rows", None),
            P("rows"),
            P("cols", "rows"),
        ),
        out_specs=(P("cols", "rows"), P("cols", "rows"), P("cols", None), P("cols")),
        check_vma=False,
    )
```

```python
import math

import jax
import jax.numpy as jnp
from jax import lax
from jax.sharding import PartitionSpec as P

BAND = 16
GROUP_ROUNDS = 2


def shifted(x, axis, size, d):
    return lax.ppermute(x, axis, [((i + d) % size, i) for i in range(size)])


def pair_join(mine, got, upper):
    return jnp.where(upper, jnp.concatenate([got, mine]), jnp.concatenate([mine, got]))


def exchange(panel, acc, row, size):
    lanes = panel.shape[-1]
    block = panel[None]
    rounds = [(0, 1)]
    low = 1
    while low < size.bit_length() - 1:
        bits = min(2, size.bit_length() - 1 - low)
        rounds.append((low, bits))
        low += bits
    for number, (low, bits) in enumerate(rounds):
        width = 1 << bits
        digit = (row >> low) % width
        carry = number < GROUP_ROUNDS
        if carry:
            flat = block.reshape(-1, lanes).astype(jnp.float32)
            send = jnp.concatenate([flat, acc])
        else:
            send = acc
        got = [send]
        for j in range(1, width):
            pairs = [(i, i ^ (j << low)) for i in range(size)]
            got.append(lax.ppermute(send, "rows", pairs))
        order = jnp.bitwise_xor(jnp.arange(width, dtype=jnp.int32), digit)
        ordered = jnp.take(jnp.stack(got), order, axis=0)
        if carry:
            rows_in = flat.shape[0]
            block = ordered[:, :rows_in].reshape((-1,) + block.shape[1:]).astype(block.dtype)
            parts = ordered[:, rows_in:]
        else:
            parts = ordered
        acc = parts[0]
        for d in range(1, width):
            acc = acc + parts[d]
    group = block.shape[0]
    table = [block]
    for m in range(1, BAND // group + 1):
        table = [shifted(block, "rows", size, -m * group)] + table
        table.append(shifted(block, "rows", size, m * group))
    return jnp.concatenate(table), acc


def band_products(table, tiles, index, mask):
    picked = jnp.take(table, index, axis=0)
    picked = jnp.where(mask[:, None, None], picked, jnp.zeros((), picked.dtype))
    return jnp.einsum("sfk,srk->fr", picked, tiles, preferred_element_type=jnp.float32)


def per_device(
    features, weight_matrix, bias_vector, adjacency_tiles, tile_cols, tile_count, out_grad
):
    feature_width, rows_here = features.shape
    rows_count = lax.axis_size("rows")
    cols_count = lax.axis_size("cols")
    assert adjacency_tiles.shape[0] == 1
    assert rows_count & (rows_count - 1) == 0 and rows_count >= 64
    assert cols_count & (cols_count - 1) == 0
    row = lax.axis_index("rows")
    col = lax.axis_index("cols")
    tiles = adjacency_tiles[0]
    column_ids = tile_cols[0]
    count = tile_count[0]
    slot_count = column_ids.shape[0]
    group = 8

    alive = jnp.arange(slot_count, dtype=jnp.int32) < count
    offset = (column_ids - row + rows_count // 2) % rows_count - rows_count // 2
    near = jnp.abs(offset) <= BAND
    is_hub = count == slot_count
    near_mask = alive & near
    far = alive & jnp.logical_not(near) & jnp.logical_not(is_hub)
    has_far = jnp.any(far)
    index = jnp.where(near, offset + row % group + BAND, BAND)
    far_slot = jnp.argmax(far)
    far_tile = lax.dynamic_index_in_dim(tiles, far_slot, 0, keepdims=False)
    far_tile = jnp.where(has_far, far_tile, jnp.zeros((), far_tile.dtype))

    def hub_terms(x):
        own = jnp.where(is_hub, x, jnp.zeros((), x.dtype)).astype(jnp.float32)
        back = jnp.einsum("fk,kr->fr", x, far_tile, preferred_element_type=jnp.float32)
        return own, back

    def finish(table, hub_panel, hub_sum):
        total = band_products(table, tiles, index, near_mask)
        total = total + jnp.einsum(
            "fk,rk->fr", hub_panel, far_tile, preferred_element_type=jnp.float32
        )
        return total + jnp.where(is_hub, hub_sum, jnp.zeros((), hub_sum.dtype))

    own, back = hub_terms(features)
    table, reduced = exchange(features, jnp.concatenate([own, back]), row, rows_count)
    hub_panel = reduced[:feature_width].astype(jnp.bfloat16)
    aggregated = finish(table, hub_panel, reduced[feature_width:]).astype(jnp.bfloat16)

    both = jnp.stack([aggregated, out_grad])
    step = 1
    while step < cols_count:
        got = lax.ppermute(both, "cols", [(i, i ^ step) for i in range(cols_count)])
        upper = (col // step) % 2 == 1
        both = jnp.where(
            upper, jnp.concatenate([got, both], axis=1), jnp.concatenate([both, got], axis=1)
        )
        step *= 2
    agg_full = both[0].reshape(-1, rows_here)
    grad_full = both[1].reshape(-1, rows_here)

    preact = (
        jnp.dot(weight_matrix, agg_full, preferred_element_type=jnp.float32)
        + bias_vector[:, None]
    )
    sigmoid_pre = jax.nn.sigmoid(preact)
    pre_grad = (
        grad_full.astype(jnp.float32) * sigmoid_pre * (1.0 + preact * (1.0 - sigmoid_pre))
    ).astype(jnp.bfloat16)
    start = col * feature_width
    own_pre = lax.dynamic_slice_in_dim(preact, start, feature_width, 0)
    own_sig = lax.dynamic_slice_in_dim(sigmoid_pre, start, feature_width, 0)
    layer_out = (own_pre * own_sig).astype(jnp.bfloat16)
    own_grad = lax.dynamic_slice_in_dim(pre_grad, start, feature_width, 0)
    weight_cols = lax.dynamic_slice_in_dim(weight_matrix, start, feature_width, 1)
    agg_grad = jnp.einsum(
        "oi,on->in", weight_cols, pre_grad, preferred_element_type=jnp.float32
    ).astype(jnp.bfloat16)
    weight_part = jnp.einsum(
        "fn,in->fi", own_grad, agg_full, preferred_element_type=jnp.float32
    )
    bias_part = jnp.sum(own_grad.astype(jnp.float32), axis=1)

    own2, back2 = hub_terms(agg_grad)
    width = weight_part.shape[1]
    lanes = rows_here
    bias_rows = jnp.zeros((8, lanes), jnp.float32).at[0, :feature_width].set(bias_part)
    packed = jnp.concatenate(
        [own2, back2, weight_part.reshape(-1, lanes), bias_rows]
    )
    table2, reduced2 = exchange(agg_grad, packed, row, rows_count)
    hub_panel2 = reduced2[:feature_width].astype(jnp.bfloat16)
    hub_sum2 = reduced2[feature_width : 2 * feature_width]
    feature_grad = finish(table2, hub_panel2, hub_sum2).astype(jnp.bfloat16)
    grad_scale = 1.0 / math.sqrt(rows_here * rows_count)
    weight_rows = feature_width * width // lanes
    weight_grad = (
        reduced2[2 * feature_width : 2 * feature_width + weight_rows].reshape(feature_width, width)
        * grad_scale
    )
    bias_grad = reduced2[2 * feature_width + weight_rows, :feature_width] * grad_scale
    return (layer_out, feature_grad, weight_grad, bias_grad)


def solution(mesh):
    return jax.shard_map(
        per_device,
        mesh=mesh,
        in_specs=(
            P("cols", "rows"),
            P(),
            P(),
            P("rows", None, None, None),
            P("rows", None),
            P("rows"),
            P("cols", "rows"),
        ),
        out_specs=(P("cols", "rows"), P("cols", "rows"), P("cols", None), P("cols")),
        check_vma=False,
    )
```

```python
import math

import jax
import jax.numpy as jnp
from jax import lax
from jax.sharding import PartitionSpec as P

BAND = 16
GROUP_ROUNDS = 2


def shifted(x, axis, size, d):
    return lax.ppermute(x, axis, [((i + d) % size, i) for i in range(size)])


def pair_join(mine, got, upper):
    return jnp.where(upper, jnp.concatenate([got, mine]), jnp.concatenate([mine, got]))


def gather_axis(x, axis):
    size = lax.axis_size(axis)
    spread = jnp.broadcast_to(x[None], (size,) + x.shape)
    return lax.all_to_all(spread, axis, 0, 0, tiled=True)


def exchange(panel, acc, rows_axes, carry_axes):
    lanes = panel.shape[-1]
    block = panel[None]
    for axis in reversed(rows_axes):
        carry = axis in carry_axes
        if carry:
            flat = block.reshape(-1, lanes).astype(jnp.float32)
            send = jnp.concatenate([flat, acc])
        else:
            send = acc
        got = gather_axis(send, axis)
        if carry:
            rows_in = flat.shape[0]
            block = got[:, :rows_in].reshape((-1,) + block.shape[1:]).astype(block.dtype)
            parts = got[:, rows_in:]
        else:
            parts = got
        acc = parts[0]
        for d in range(1, parts.shape[0]):
            acc = acc + parts[d]
    group = block.shape[0]
    size = lax.axis_size(rows_axes)
    table = [block]
    for m in range(1, BAND // group + 1):
        table = [shifted(block, rows_axes, size, -m * group)] + table
        table.append(shifted(block, rows_axes, size, m * group))
    return jnp.concatenate(table), acc


def band_products(table, tiles, index, mask):
    picked = jnp.take(table, index, axis=0)
    picked = jnp.where(mask[:, None, None], picked, jnp.zeros((), picked.dtype))
    return jnp.einsum("sfk,srk->fr", picked, tiles, preferred_element_type=jnp.float32)


def per_device(
    features, weight_matrix, bias_vector, adjacency_tiles, tile_cols, tile_count, out_grad
):
    feature_width, rows_here = features.shape
    rows_count = lax.axis_size(ROWS)
    cols_count = lax.axis_size("cols")
    assert adjacency_tiles.shape[0] == 1
    assert rows_count & (rows_count - 1) == 0 and rows_count >= 64
    assert cols_count & (cols_count - 1) == 0
    row = lax.axis_index(ROWS)
    col = lax.axis_index("cols")
    tiles = adjacency_tiles[0]
    column_ids = tile_cols[0]
    count = tile_count[0]
    slot_count = column_ids.shape[0]
    group = 8

    alive = jnp.arange(slot_count, dtype=jnp.int32) < count
    offset = (column_ids - row + rows_count // 2) % rows_count - rows_count // 2
    near = jnp.abs(offset) <= BAND
    is_hub = count == slot_count
    near_mask = alive & near
    far = alive & jnp.logical_not(near) & jnp.logical_not(is_hub)
    has_far = jnp.any(far)
    index = jnp.where(near, offset + row % group + BAND, BAND)
    far_slot = jnp.argmax(far)
    far_tile = lax.dynamic_index_in_dim(tiles, far_slot, 0, keepdims=False)
    far_tile = jnp.where(has_far, far_tile, jnp.zeros((), far_tile.dtype))

    def hub_terms(x):
        own = jnp.where(is_hub, x, jnp.zeros((), x.dtype)).astype(jnp.float32)
        back = jnp.einsum("fk,kr->fr", x, far_tile, preferred_element_type=jnp.float32)
        return own, back

    def finish(table, hub_panel, hub_sum):
        total = band_products(table, tiles, index, near_mask)
        total = total + jnp.einsum(
            "fk,rk->fr", hub_panel, far_tile, preferred_element_type=jnp.float32
        )
        return total + jnp.where(is_hub, hub_sum, jnp.zeros((), hub_sum.dtype))

    own, back = hub_terms(features)
    table, reduced = exchange(features, jnp.concatenate([own, back]), ROWS, CARRY)
    hub_panel = reduced[:feature_width].astype(jnp.bfloat16)
    aggregated = finish(table, hub_panel, reduced[feature_width:]).astype(jnp.bfloat16)

    both = gather_axis(jnp.stack([aggregated, out_grad]), "cols")
    both = jnp.swapaxes(both, 0, 1)
    agg_full = both[0].reshape(-1, rows_here)
    grad_full = both[1].reshape(-1, rows_here)

    preact = (
        jnp.dot(weight_matrix, agg_full, preferred_element_type=jnp.float32)
        + bias_vector[:, None]
    )
    sigmoid_pre = jax.nn.sigmoid(preact)
    pre_grad = (
        grad_full.astype(jnp.float32) * sigmoid_pre * (1.0 + preact * (1.0 - sigmoid_pre))
    ).astype(jnp.bfloat16)
    start = col * feature_width
    own_pre = lax.dynamic_slice_in_dim(preact, start, feature_width, 0)
    own_sig = lax.dynamic_slice_in_dim(sigmoid_pre, start, feature_width, 0)
    layer_out = (own_pre * own_sig).astype(jnp.bfloat16)
    own_grad = lax.dynamic_slice_in_dim(pre_grad, start, feature_width, 0)
    weight_cols = lax.dynamic_slice_in_dim(weight_matrix, start, feature_width, 1)
    agg_grad = jnp.einsum(
        "oi,on->in", weight_cols, pre_grad, preferred_element_type=jnp.float32
    ).astype(jnp.bfloat16)
    weight_part = jnp.einsum(
        "fn,in->fi", own_grad, agg_full, preferred_element_type=jnp.float32
    )
    bias_part = jnp.sum(own_grad.astype(jnp.float32), axis=1)

    own2, back2 = hub_terms(agg_grad)
    width = weight_part.shape[1]
    lanes = rows_here
    bias_rows = jnp.zeros((8, lanes), jnp.float32).at[0, :feature_width].set(bias_part)
    packed = jnp.concatenate(
        [own2, back2, weight_part.reshape(-1, lanes), bias_rows]
    )
    table2, reduced2 = exchange(agg_grad, packed, ROWS, CARRY)
    hub_panel2 = reduced2[:feature_width].astype(jnp.bfloat16)
    hub_sum2 = reduced2[feature_width : 2 * feature_width]
    feature_grad = finish(table2, hub_panel2, hub_sum2).astype(jnp.bfloat16)
    grad_scale = 1.0 / math.sqrt(rows_here * rows_count)
    weight_rows = feature_width * width // lanes
    weight_grad = (
        reduced2[2 * feature_width : 2 * feature_width + weight_rows].reshape(feature_width, width)
        * grad_scale
    )
    bias_grad = reduced2[2 * feature_width + weight_rows, :feature_width] * grad_scale
    return (layer_out, feature_grad, weight_grad, bias_grad)


ROWS = ("zh", "zl", "y", "core")
CARRY = ("y", "core")


def solution(mesh):
    rows_count = mesh.shape["rows"]
    cols_count = mesh.shape["cols"]
    assert rows_count % 32 == 0
    split = jax.sharding.Mesh(
        mesh.devices.reshape(rows_count // 32, 4, 4, 2, cols_count), ROWS + ("cols",)
    )
    return jax.shard_map(
        per_device,
        mesh=split,
        in_specs=(
            P("cols", ROWS),
            P(),
            P(),
            P(ROWS, None, None, None),
            P(ROWS, None),
            P(ROWS),
            P("cols", ROWS),
        ),
        out_specs=(P("cols", ROWS), P("cols", ROWS), P("cols", None), P("cols")),
        check_vma=False,
    )
```

```python
import math

import jax
import jax.numpy as jnp
from jax import lax
from jax.sharding import PartitionSpec as P

BAND = 16
GROUP_ROUNDS = 2


def shifted(x, axis, size, d):
    return lax.ppermute(x, axis, [((i + d) % size, i) for i in range(size)])


def pair_join(mine, got, upper):
    return jnp.where(upper, jnp.concatenate([got, mine]), jnp.concatenate([mine, got]))


def gather_axis(x, axis):
    size = lax.axis_size(axis)
    spread = jnp.broadcast_to(x[None], (size,) + x.shape)
    return lax.all_to_all(spread, axis, 0, 0, tiled=True)


def exchange(panel, acc, rows_axes, carry_axes):
    lanes = panel.shape[-1]
    block = panel[None]
    for axis in reversed(rows_axes):
        carry = axis in carry_axes
        if carry:
            flat = block.reshape(-1, lanes).astype(jnp.float32)
            send = jnp.concatenate([flat, acc])
        else:
            send = acc
        got = gather_axis(send, axis)
        if carry:
            rows_in = flat.shape[0]
            block = got[:, :rows_in].reshape((-1,) + block.shape[1:]).astype(block.dtype)
            parts = got[:, rows_in:]
        else:
            parts = got
        acc = parts[0]
        for d in range(1, parts.shape[0]):
            acc = acc + parts[d]
    group = block.shape[0]
    size = lax.axis_size(rows_axes)
    table = [block]
    for m in range(1, BAND // group + 1):
        table = [shifted(block, rows_axes, size, -m * group)] + table
        table.append(shifted(block, rows_axes, size, m * group))
    return jnp.concatenate(table), acc


def band_products(table, tiles, index, mask):
    picked = jnp.take(table, index, axis=0)
    picked = jnp.where(mask[:, None, None], picked, jnp.zeros((), picked.dtype))
    return jnp.einsum("sfk,srk->fr", picked, tiles, preferred_element_type=jnp.float32)


def per_device(
    features, weight_matrix, bias_vector, adjacency_tiles, tile_cols, tile_count, out_grad
):
    feature_width, rows_here = features.shape
    rows_count = lax.axis_size(ROWS)
    cols_count = lax.axis_size("cols")
    assert adjacency_tiles.shape[0] == 1
    assert rows_count & (rows_count - 1) == 0 and rows_count >= 64
    assert cols_count & (cols_count - 1) == 0
    row = lax.axis_index(ROWS)
    col = lax.axis_index("cols")
    tiles = adjacency_tiles[0]
    column_ids = tile_cols[0]
    count = tile_count[0]
    slot_count = column_ids.shape[0]
    group = 8

    alive = jnp.arange(slot_count, dtype=jnp.int32) < count
    offset = (column_ids - row + rows_count // 2) % rows_count - rows_count // 2
    near = jnp.abs(offset) <= BAND
    is_hub = count == slot_count
    near_mask = alive & near
    far = alive & jnp.logical_not(near) & jnp.logical_not(is_hub)
    has_far = jnp.any(far)
    index = jnp.where(near, offset + row % group + BAND, BAND)
    far_slot = jnp.argmax(far)
    far_tile = lax.dynamic_index_in_dim(tiles, far_slot, 0, keepdims=False)
    far_tile = jnp.where(has_far, far_tile, jnp.zeros((), far_tile.dtype))

    def hub_terms(x):
        own = jnp.where(is_hub, x, jnp.zeros((), x.dtype)).astype(jnp.float32)
        back = jnp.einsum("fk,kr->fr", x, far_tile, preferred_element_type=jnp.float32)
        return own, back

    def finish(table, hub_panel, hub_sum):
        total = band_products(table, tiles, index, near_mask)
        total = total + jnp.einsum(
            "fk,rk->fr", hub_panel, far_tile, preferred_element_type=jnp.float32
        )
        return total + jnp.where(is_hub, hub_sum, jnp.zeros((), hub_sum.dtype))

    own, back = hub_terms(features)
    table, reduced = exchange(features, jnp.concatenate([own, back]), ROWS, CARRY)
    hub_panel = reduced[:feature_width].astype(jnp.bfloat16)
    aggregated = finish(table, hub_panel, reduced[feature_width:]).astype(jnp.bfloat16)

    both = gather_axis(jnp.stack([aggregated, out_grad]), "cols")
    both = jnp.swapaxes(both, 0, 1)
    agg_full = both[0].reshape(-1, rows_here)
    grad_full = both[1].reshape(-1, rows_here)

    preact = (
        jnp.dot(weight_matrix, agg_full, preferred_element_type=jnp.float32)
        + bias_vector[:, None]
    )
    sigmoid_pre = jax.nn.sigmoid(preact)
    pre_grad = (
        grad_full.astype(jnp.float32) * sigmoid_pre * (1.0 + preact * (1.0 - sigmoid_pre))
    ).astype(jnp.bfloat16)
    start = col * feature_width
    own_pre = lax.dynamic_slice_in_dim(preact, start, feature_width, 0)
    own_sig = lax.dynamic_slice_in_dim(sigmoid_pre, start, feature_width, 0)
    layer_out = (own_pre * own_sig).astype(jnp.bfloat16)
    own_grad = lax.dynamic_slice_in_dim(pre_grad, start, feature_width, 0)
    weight_cols = lax.dynamic_slice_in_dim(weight_matrix, start, feature_width, 1)
    agg_grad = jnp.einsum(
        "oi,on->in", weight_cols, pre_grad, preferred_element_type=jnp.float32
    ).astype(jnp.bfloat16)
    weight_part = jnp.einsum(
        "fn,in->fi", own_grad, agg_full, preferred_element_type=jnp.float32
    )
    bias_part = jnp.sum(own_grad.astype(jnp.float32), axis=1)

    own2, back2 = hub_terms(agg_grad)
    width = weight_part.shape[1]
    bias_row = jnp.zeros((1, width), jnp.float32).at[0, :feature_width].set(bias_part)
    sums = jnp.concatenate([weight_part, bias_row])
    for axis in reversed(ROWS):
        sums = lax.optimization_barrier(lax.psum(sums, axis))
    packed = jnp.concatenate([own2, back2])
    table2, reduced2 = exchange(agg_grad, packed, ROWS, CARRY)
    hub_panel2 = reduced2[:feature_width].astype(jnp.bfloat16)
    hub_sum2 = reduced2[feature_width : 2 * feature_width]
    feature_grad = finish(table2, hub_panel2, hub_sum2).astype(jnp.bfloat16)
    grad_scale = 1.0 / math.sqrt(rows_here * rows_count)
    weight_grad = sums[:feature_width] * grad_scale
    bias_grad = sums[feature_width, :feature_width] * grad_scale
    return (layer_out, feature_grad, weight_grad, bias_grad)


ROWS = ("zh", "zl", "y", "core")
CARRY = ("y", "core")


def solution(mesh):
    rows_count = mesh.shape["rows"]
    cols_count = mesh.shape["cols"]
    assert rows_count % 32 == 0
    split = jax.sharding.Mesh(
        mesh.devices.reshape(rows_count // 32, 4, 4, 2, cols_count), ROWS + ("cols",)
    )
    return jax.shard_map(
        per_device,
        mesh=split,
        in_specs=(
            P("cols", ROWS),
            P(),
            P(),
            P(ROWS, None, None, None),
            P(ROWS, None),
            P(ROWS),
            P("cols", ROWS),
        ),
        out_specs=(P("cols", ROWS), P("cols", ROWS), P("cols", None), P("cols")),
        check_vma=False,
    )
```

```python
import math

import jax
import jax.numpy as jnp
from jax import lax
from jax.sharding import PartitionSpec as P

BAND = 16
GROUP_ROUNDS = 2


def shifted(x, axis, size, d):
    return lax.ppermute(x, axis, [((i + d) % size, i) for i in range(size)])


def pair_join(mine, got, upper):
    return jnp.where(upper, jnp.concatenate([got, mine]), jnp.concatenate([mine, got]))


def gather_axis(x, axis):
    size = lax.axis_size(axis)
    spread = jnp.broadcast_to(x[None], (size,) + x.shape)
    return lax.all_to_all(spread, axis, 0, 0, tiled=True)


def exchange(panel, acc, rows_axes, carry_axes):
    lanes = panel.shape[-1]
    block = panel[None]
    for axis in ROUNDS:
        carry = axis in carry_axes
        if carry:
            flat = block.reshape(-1, lanes).astype(jnp.float32)
            send = jnp.concatenate([flat, acc])
        else:
            send = acc
        got = gather_axis(send, axis)
        if carry:
            rows_in = flat.shape[0]
            block = got[:, :rows_in].reshape((-1,) + block.shape[1:]).astype(block.dtype)
            parts = got[:, rows_in:]
        else:
            parts = got
        acc = parts[0]
        for d in range(1, parts.shape[0]):
            acc = acc + parts[d]
    group = block.shape[0]
    size = lax.axis_size(rows_axes)
    table = [block]
    for m in range(1, BAND // group + 1):
        table = [shifted(block, rows_axes, size, -m * group)] + table
        table.append(shifted(block, rows_axes, size, m * group))
    return jnp.concatenate(table), acc


def band_products(table, tiles, index, mask):
    picked = jnp.take(table, index, axis=0)
    picked = jnp.where(mask[:, None, None], picked, jnp.zeros((), picked.dtype))
    return jnp.einsum("sfk,srk->fr", picked, tiles, preferred_element_type=jnp.float32)


def per_device(
    features, weight_matrix, bias_vector, adjacency_tiles, tile_cols, tile_count, out_grad
):
    feature_width, rows_here = features.shape
    rows_count = lax.axis_size(ROWS)
    cols_count = lax.axis_size("cols")
    assert adjacency_tiles.shape[0] == 1
    assert rows_count & (rows_count - 1) == 0 and rows_count >= 64
    assert cols_count & (cols_count - 1) == 0
    row = lax.axis_index(ROWS)
    col = lax.axis_index("cols")
    tiles = adjacency_tiles[0]
    column_ids = tile_cols[0]
    count = tile_count[0]
    slot_count = column_ids.shape[0]
    group = 8

    alive = jnp.arange(slot_count, dtype=jnp.int32) < count
    offset = (column_ids - row + rows_count // 2) % rows_count - rows_count // 2
    near = jnp.abs(offset) <= BAND
    is_hub = count == slot_count
    near_mask = alive & near
    far = alive & jnp.logical_not(near) & jnp.logical_not(is_hub)
    has_far = jnp.any(far)
    index = jnp.where(near, offset + row % group + BAND, BAND)
    far_slot = jnp.argmax(far)
    far_tile = lax.dynamic_index_in_dim(tiles, far_slot, 0, keepdims=False)
    far_tile = jnp.where(has_far, far_tile, jnp.zeros((), far_tile.dtype))

    def hub_terms(x):
        own = jnp.where(is_hub, x, jnp.zeros((), x.dtype)).astype(jnp.float32)
        back = jnp.einsum("fk,kr->fr", x, far_tile, preferred_element_type=jnp.float32)
        return own, back

    def finish(table, hub_panel, hub_sum):
        total = band_products(table, tiles, index, near_mask)
        total = total + jnp.einsum(
            "fk,rk->fr", hub_panel, far_tile, preferred_element_type=jnp.float32
        )
        return total + jnp.where(is_hub, hub_sum, jnp.zeros((), hub_sum.dtype))

    own, back = hub_terms(features)
    table, reduced = exchange(features, jnp.concatenate([own, back]), ROWS, CARRY)
    hub_panel = reduced[:feature_width].astype(jnp.bfloat16)
    aggregated = finish(table, hub_panel, reduced[feature_width:]).astype(jnp.bfloat16)

    both = gather_axis(jnp.stack([aggregated, out_grad]), "cols")
    both = jnp.swapaxes(both, 0, 1)
    agg_full = both[0].reshape(-1, rows_here)
    grad_full = both[1].reshape(-1, rows_here)

    preact = (
        jnp.dot(weight_matrix, agg_full, preferred_element_type=jnp.float32)
        + bias_vector[:, None]
    )
    sigmoid_pre = jax.nn.sigmoid(preact)
    pre_grad = (
        grad_full.astype(jnp.float32) * sigmoid_pre * (1.0 + preact * (1.0 - sigmoid_pre))
    ).astype(jnp.bfloat16)
    start = col * feature_width
    own_pre = lax.dynamic_slice_in_dim(preact, start, feature_width, 0)
    own_sig = lax.dynamic_slice_in_dim(sigmoid_pre, start, feature_width, 0)
    layer_out = (own_pre * own_sig).astype(jnp.bfloat16)
    own_grad = lax.dynamic_slice_in_dim(pre_grad, start, feature_width, 0)
    weight_cols = lax.dynamic_slice_in_dim(weight_matrix, start, feature_width, 1)
    agg_grad = jnp.einsum(
        "oi,on->in", weight_cols, pre_grad, preferred_element_type=jnp.float32
    ).astype(jnp.bfloat16)
    weight_part = jnp.einsum(
        "fn,in->fi", own_grad, agg_full, preferred_element_type=jnp.float32
    )
    bias_part = jnp.sum(own_grad.astype(jnp.float32), axis=1)

    own2, back2 = hub_terms(agg_grad)
    width = weight_part.shape[1]
    lanes = rows_here
    bias_rows = jnp.zeros((8, lanes), jnp.float32).at[0, :feature_width].set(bias_part)
    packed = jnp.concatenate(
        [own2, back2, weight_part.reshape(-1, lanes), bias_rows]
    )
    table2, reduced2 = exchange(agg_grad, packed, ROWS, CARRY)
    hub_panel2 = reduced2[:feature_width].astype(jnp.bfloat16)
    hub_sum2 = reduced2[feature_width : 2 * feature_width]
    feature_grad = finish(table2, hub_panel2, hub_sum2).astype(jnp.bfloat16)
    grad_scale = 1.0 / math.sqrt(rows_here * rows_count)
    weight_rows = feature_width * width // lanes
    weight_grad = (
        reduced2[2 * feature_width : 2 * feature_width + weight_rows].reshape(feature_width, width)
        * grad_scale
    )
    bias_grad = reduced2[2 * feature_width + weight_rows, :feature_width] * grad_scale
    return (layer_out, feature_grad, weight_grad, bias_grad)


ROWS = ("zh", "zl", "y", "core")
CARRY = (("y", "core"),)
ROUNDS = (("y", "core"), "zl", "zh")


def solution(mesh):
    rows_count = mesh.shape["rows"]
    cols_count = mesh.shape["cols"]
    assert rows_count % 32 == 0
    split = jax.sharding.Mesh(
        mesh.devices.reshape(rows_count // 32, 4, 4, 2, cols_count), ROWS + ("cols",)
    )
    return jax.shard_map(
        per_device,
        mesh=split,
        in_specs=(
            P("cols", ROWS),
            P(),
            P(),
            P(ROWS, None, None, None),
            P(ROWS, None),
            P(ROWS),
            P("cols", ROWS),
        ),
        out_specs=(P("cols", ROWS), P("cols", ROWS), P("cols", None), P("cols")),
        check_vma=False,
    )
```

```python
import math

import jax
import jax.numpy as jnp
from jax import lax
from jax.sharding import PartitionSpec as P

BAND = 16
GROUP_ROUNDS = 2


def shifted(x, axis, size, d):
    return lax.ppermute(x, axis, [((i + d) % size, i) for i in range(size)])


def pair_join(mine, got, upper):
    return jnp.where(upper, jnp.concatenate([got, mine]), jnp.concatenate([mine, got]))


def gather_axis(x, axis):
    size = lax.axis_size(axis)
    spread = jnp.broadcast_to(x[None], (size,) + x.shape)
    return lax.all_to_all(spread, axis, 0, 0, tiled=True)


def exchange(panel, acc, rows_axes, carry_axes):
    lanes = panel.shape[-1]
    block = panel[None]
    for axis in reversed(rows_axes):
        carry = axis in carry_axes
        if carry:
            flat = block.reshape(-1, lanes).astype(jnp.float32)
            send = jnp.concatenate([flat, acc])
        else:
            send = acc
        got = gather_axis(send, axis)
        if carry:
            rows_in = flat.shape[0]
            block = got[:, :rows_in].reshape((-1,) + block.shape[1:]).astype(block.dtype)
            parts = got[:, rows_in:]
        else:
            parts = got
        acc = parts[0]
        for d in range(1, parts.shape[0]):
            acc = acc + parts[d]
    group = block.shape[0]
    half = group // 2
    assert half == BAND
    size = lax.axis_size(rows_axes)
    lower = lax.axis_index(rows_axes) % group < half
    pairs = [(i, (i + group) % size if i % group < half else (i - group) % size) for i in range(size)]
    send = jnp.where(lower, block[half:], block[:half])
    got = lax.ppermute(send, rows_axes, pairs)
    table = jnp.where(lower, jnp.concatenate([got, block]), jnp.concatenate([block, got]))
    return table, acc


def band_products(table, tiles, index, mask):
    picked = jnp.take(table, index, axis=0)
    picked = jnp.where(mask[:, None, None], picked, jnp.zeros((), picked.dtype))
    return jnp.einsum("sfk,srk->fr", picked, tiles, preferred_element_type=jnp.float32)


def per_device(
    features, weight_matrix, bias_vector, adjacency_tiles, tile_cols, tile_count, out_grad
):
    feature_width, rows_here = features.shape
    rows_count = lax.axis_size(ROWS)
    cols_count = lax.axis_size("cols")
    assert adjacency_tiles.shape[0] == 1
    assert rows_count & (rows_count - 1) == 0 and rows_count >= 64
    assert cols_count & (cols_count - 1) == 0
    row = lax.axis_index(ROWS)
    col = lax.axis_index("cols")
    tiles = adjacency_tiles[0]
    column_ids = tile_cols[0]
    count = tile_count[0]
    slot_count = column_ids.shape[0]
    group = 2 * BAND

    alive = jnp.arange(slot_count, dtype=jnp.int32) < count
    offset = (column_ids - row + rows_count // 2) % rows_count - rows_count // 2
    near = jnp.abs(offset) <= BAND
    is_hub = count == slot_count
    near_mask = alive & near
    far = alive & jnp.logical_not(near) & jnp.logical_not(is_hub)
    has_far = jnp.any(far)
    place = row % group
    index = jnp.where(near, offset + place + jnp.where(place < BAND, BAND, 0), BAND)
    far_slot = jnp.argmax(far)
    far_tile = lax.dynamic_index_in_dim(tiles, far_slot, 0, keepdims=False)
    far_tile = jnp.where(has_far, far_tile, jnp.zeros((), far_tile.dtype))

    def hub_terms(x):
        own = jnp.where(is_hub, x, jnp.zeros((), x.dtype)).astype(jnp.float32)
        back = jnp.einsum("fk,kr->fr", x, far_tile, preferred_element_type=jnp.float32)
        return own, back

    def finish(table, hub_panel, hub_sum):
        total = band_products(table, tiles, index, near_mask)
        total = total + jnp.einsum(
            "fk,rk->fr", hub_panel, far_tile, preferred_element_type=jnp.float32
        )
        return total + jnp.where(is_hub, hub_sum, jnp.zeros((), hub_sum.dtype))

    own, back = hub_terms(features)
    table, reduced = exchange(features, jnp.concatenate([own, back]), ROWS, CARRY)
    hub_panel = reduced[:feature_width].astype(jnp.bfloat16)
    aggregated = finish(table, hub_panel, reduced[feature_width:]).astype(jnp.bfloat16)

    both = gather_axis(jnp.stack([aggregated, out_grad]), "cols")
    both = jnp.swapaxes(both, 0, 1)
    agg_full = both[0].reshape(-1, rows_here)
    grad_full = both[1].reshape(-1, rows_here)

    preact = (
        jnp.dot(weight_matrix, agg_full, preferred_element_type=jnp.float32)
        + bias_vector[:, None]
    )
    sigmoid_pre = jax.nn.sigmoid(preact)
    pre_grad = (
        grad_full.astype(jnp.float32) * sigmoid_pre * (1.0 + preact * (1.0 - sigmoid_pre))
    ).astype(jnp.bfloat16)
    start = col * feature_width
    own_pre = lax.dynamic_slice_in_dim(preact, start, feature_width, 0)
    own_sig = lax.dynamic_slice_in_dim(sigmoid_pre, start, feature_width, 0)
    layer_out = (own_pre * own_sig).astype(jnp.bfloat16)
    own_grad = lax.dynamic_slice_in_dim(pre_grad, start, feature_width, 0)
    weight_cols = lax.dynamic_slice_in_dim(weight_matrix, start, feature_width, 1)
    agg_grad = jnp.einsum(
        "oi,on->in", weight_cols, pre_grad, preferred_element_type=jnp.float32
    ).astype(jnp.bfloat16)
    weight_part = jnp.einsum(
        "fn,in->fi", own_grad, agg_full, preferred_element_type=jnp.float32
    )
    bias_part = jnp.sum(own_grad.astype(jnp.float32), axis=1)

    own2, back2 = hub_terms(agg_grad)
    width = weight_part.shape[1]
    lanes = rows_here
    bias_rows = jnp.zeros((8, lanes), jnp.float32).at[0, :feature_width].set(bias_part)
    packed = jnp.concatenate(
        [own2, back2, weight_part.reshape(-1, lanes), bias_rows]
    )
    table2, reduced2 = exchange(agg_grad, packed, ROWS, CARRY)
    hub_panel2 = reduced2[:feature_width].astype(jnp.bfloat16)
    hub_sum2 = reduced2[feature_width : 2 * feature_width]
    feature_grad = finish(table2, hub_panel2, hub_sum2).astype(jnp.bfloat16)
    grad_scale = 1.0 / math.sqrt(rows_here * rows_count)
    weight_rows = feature_width * width // lanes
    weight_grad = (
        reduced2[2 * feature_width : 2 * feature_width + weight_rows].reshape(feature_width, width)
        * grad_scale
    )
    bias_grad = reduced2[2 * feature_width + weight_rows, :feature_width] * grad_scale
    return (layer_out, feature_grad, weight_grad, bias_grad)


ROWS = ("zh", "zl", "y", "core")
CARRY = ("zl", "y", "core")


def solution(mesh):
    rows_count = mesh.shape["rows"]
    cols_count = mesh.shape["cols"]
    assert rows_count % 32 == 0
    split = jax.sharding.Mesh(
        mesh.devices.reshape(rows_count // 32, 4, 4, 2, cols_count), ROWS + ("cols",)
    )
    return jax.shard_map(
        per_device,
        mesh=split,
        in_specs=(
            P("cols", ROWS),
            P(),
            P(),
            P(ROWS, None, None, None),
            P(ROWS, None),
            P(ROWS),
            P("cols", ROWS),
        ),
        out_specs=(P("cols", ROWS), P("cols", ROWS), P("cols", None), P("cols")),
        check_vma=False,
    )
```

```python
import math

import jax
import jax.numpy as jnp
from jax import lax
from jax.sharding import PartitionSpec as P

BAND = 16
GROUP_ROUNDS = 2


def shifted(x, axis, size, d):
    return lax.ppermute(x, axis, [((i + d) % size, i) for i in range(size)])


def pair_join(mine, got, upper):
    return jnp.where(upper, jnp.concatenate([got, mine]), jnp.concatenate([mine, got]))


def gather_axis(x, axis):
    size = lax.axis_size(axis)
    spread = jnp.broadcast_to(x[None], (size,) + x.shape)
    return lax.all_to_all(spread, axis, 0, 0, tiled=True)


def exchange(panel, acc, rows_axes, carry_axes, rounds):
    lanes = panel.shape[-1]
    block = panel[None]
    for axis in rounds:
        carry = axis in carry_axes
        if carry:
            flat = block.reshape(-1, lanes).astype(jnp.float32)
            send = jnp.concatenate([flat, acc])
        else:
            send = acc
        got = gather_axis(send, axis)
        if carry:
            rows_in = flat.shape[0]
            block = got[:, :rows_in].reshape((-1,) + block.shape[1:]).astype(block.dtype)
            parts = got[:, rows_in:]
        else:
            parts = got
        acc = parts[0]
        for d in range(1, parts.shape[0]):
            acc = acc + parts[d]
    group = block.shape[0]
    size = lax.axis_size(rows_axes)
    table = [block]
    for m in range(1, BAND // group + 1):
        table = [shifted(block, rows_axes, size, -m * group)] + table
        table.append(shifted(block, rows_axes, size, m * group))
    return jnp.concatenate(table), acc


def band_products(table, tiles, index, mask):
    picked = jnp.take(table, index, axis=0)
    picked = jnp.where(mask[:, None, None], picked, jnp.zeros((), picked.dtype))
    return jnp.einsum("sfk,srk->fr", picked, tiles, preferred_element_type=jnp.float32)


def per_device(
    features, weight_matrix, bias_vector, adjacency_tiles, tile_cols, tile_count, out_grad
):
    feature_width, rows_here = features.shape
    rows_count = lax.axis_size(ROWS)
    cols_count = lax.axis_size("cols")
    assert adjacency_tiles.shape[0] == 1
    assert rows_count & (rows_count - 1) == 0 and rows_count >= 64
    assert cols_count & (cols_count - 1) == 0
    row = lax.axis_index(ROWS)
    col = lax.axis_index("cols")
    tiles = adjacency_tiles[0]
    column_ids = tile_cols[0]
    count = tile_count[0]
    slot_count = column_ids.shape[0]
    group = 8

    alive = jnp.arange(slot_count, dtype=jnp.int32) < count
    offset = (column_ids - row + rows_count // 2) % rows_count - rows_count // 2
    near = jnp.abs(offset) <= BAND
    is_hub = count == slot_count
    near_mask = alive & near
    far = alive & jnp.logical_not(near) & jnp.logical_not(is_hub)
    has_far = jnp.any(far)
    index = jnp.where(near, offset + row % group + BAND, BAND)
    far_slot = jnp.argmax(far)
    far_tile = lax.dynamic_index_in_dim(tiles, far_slot, 0, keepdims=False)
    far_tile = jnp.where(has_far, far_tile, jnp.zeros((), far_tile.dtype))

    def hub_terms(x):
        own = jnp.where(is_hub, x, jnp.zeros((), x.dtype)).astype(jnp.float32)
        back = jnp.einsum("fk,kr->fr", x, far_tile, preferred_element_type=jnp.float32)
        return own, back

    def finish(table, hub_panel, hub_sum):
        total = band_products(table, tiles, index, near_mask)
        total = total + jnp.einsum(
            "fk,rk->fr", hub_panel, far_tile, preferred_element_type=jnp.float32
        )
        return total + jnp.where(is_hub, hub_sum, jnp.zeros((), hub_sum.dtype))

    own, back = hub_terms(features)
    table, reduced = exchange(
        features, jnp.concatenate([own, back]), ROWS, ((("y", "core")),), (("y", "core"), "zl", "zh")
    )
    hub_panel = reduced[:feature_width].astype(jnp.bfloat16)
    aggregated = finish(table, hub_panel, reduced[feature_width:]).astype(jnp.bfloat16)

    both = gather_axis(jnp.stack([aggregated, out_grad]), "cols")
    both = jnp.swapaxes(both, 0, 1)
    agg_full = both[0].reshape(-1, rows_here)
    grad_full = both[1].reshape(-1, rows_here)

    preact = (
        jnp.dot(weight_matrix, agg_full, preferred_element_type=jnp.float32)
        + bias_vector[:, None]
    )
    sigmoid_pre = jax.nn.sigmoid(preact)
    pre_grad = (
        grad_full.astype(jnp.float32) * sigmoid_pre * (1.0 + preact * (1.0 - sigmoid_pre))
    ).astype(jnp.bfloat16)
    start = col * feature_width
    own_pre = lax.dynamic_slice_in_dim(preact, start, feature_width, 0)
    own_sig = lax.dynamic_slice_in_dim(sigmoid_pre, start, feature_width, 0)
    layer_out = (own_pre * own_sig).astype(jnp.bfloat16)
    own_grad = lax.dynamic_slice_in_dim(pre_grad, start, feature_width, 0)
    weight_cols = lax.dynamic_slice_in_dim(weight_matrix, start, feature_width, 1)
    agg_grad = jnp.einsum(
        "oi,on->in", weight_cols, pre_grad, preferred_element_type=jnp.float32
    ).astype(jnp.bfloat16)
    weight_part = jnp.einsum(
        "fn,in->fi", own_grad, agg_full, preferred_element_type=jnp.float32
    )
    bias_part = jnp.sum(own_grad.astype(jnp.float32), axis=1)

    own2, back2 = hub_terms(agg_grad)
    width = weight_part.shape[1]
    lanes = rows_here
    bias_rows = jnp.zeros((8, lanes), jnp.float32).at[0, :feature_width].set(bias_part)
    packed = jnp.concatenate(
        [own2, back2, weight_part.reshape(-1, lanes), bias_rows]
    )
    table2, reduced2 = exchange(agg_grad, packed, ROWS, CARRY, tuple(reversed(ROWS)))
    hub_panel2 = reduced2[:feature_width].astype(jnp.bfloat16)
    hub_sum2 = reduced2[feature_width : 2 * feature_width]
    feature_grad = finish(table2, hub_panel2, hub_sum2).astype(jnp.bfloat16)
    grad_scale = 1.0 / math.sqrt(rows_here * rows_count)
    weight_rows = feature_width * width // lanes
    weight_grad = (
        reduced2[2 * feature_width : 2 * feature_width + weight_rows].reshape(feature_width, width)
        * grad_scale
    )
    bias_grad = reduced2[2 * feature_width + weight_rows, :feature_width] * grad_scale
    return (layer_out, feature_grad, weight_grad, bias_grad)


ROWS = ("zh", "zl", "y", "core")
CARRY = ("y", "core")


def solution(mesh):
    rows_count = mesh.shape["rows"]
    cols_count = mesh.shape["cols"]
    assert rows_count % 32 == 0
    split = jax.sharding.Mesh(
        mesh.devices.reshape(rows_count // 32, 4, 4, 2, cols_count), ROWS + ("cols",)
    )
    return jax.shard_map(
        per_device,
        mesh=split,
        in_specs=(
            P("cols", ROWS),
            P(),
            P(),
            P(ROWS, None, None, None),
            P(ROWS, None),
            P(ROWS),
            P("cols", ROWS),
        ),
        out_specs=(P("cols", ROWS), P("cols", ROWS), P("cols", None), P("cols")),
        check_vma=False,
    )
```

```python
import math

import jax
import jax.numpy as jnp
from jax import lax
from jax.sharding import PartitionSpec as P

BAND = 16
GROUP_ROUNDS = 2


def shifted(x, axis, size, d):
    return lax.ppermute(x, axis, [((i + d) % size, i) for i in range(size)])


def pair_join(mine, got, upper):
    return jnp.where(upper, jnp.concatenate([got, mine]), jnp.concatenate([mine, got]))


def gather_axis(x, axis):
    size = lax.axis_size(axis)
    spread = jnp.broadcast_to(x[None], (size,) + x.shape)
    return lax.all_to_all(spread, axis, 0, 0, tiled=True)


def exchange(panel, acc, rows_axes, carry_axes, split=False):
    lanes = panel.shape[-1]
    block = panel[None]
    axes = list(reversed(rows_axes))
    if split:
        core_axis = axes.pop(0)
        second = lax.axis_index(core_axis) == 1
        swap = [(0, 1), (1, 0)]
        half = acc.shape[0] // 2
        mine = jnp.where(second, acc[half:], acc[:half])
        other = jnp.where(second, acc[:half], acc[half:])
        flat = block.reshape(-1, lanes).astype(jnp.float32)
        got = lax.ppermute(jnp.concatenate([flat, other]), core_axis, swap)
        got_block = got[: flat.shape[0]].reshape(block.shape).astype(block.dtype)
        block = pair_join(block, got_block, second)
        acc = mine + got[flat.shape[0] :]
    for axis in axes:
        carry = axis in carry_axes
        if carry:
            flat = block.reshape(-1, lanes).astype(jnp.float32)
            send = jnp.concatenate([flat, acc])
        else:
            send = acc
        got = gather_axis(send, axis)
        if carry:
            rows_in = flat.shape[0]
            block = got[:, :rows_in].reshape((-1,) + block.shape[1:]).astype(block.dtype)
            parts = got[:, rows_in:]
        else:
            parts = got
        acc = parts[0]
        for d in range(1, parts.shape[0]):
            acc = acc + parts[d]
    if split:
        got = lax.ppermute(acc, core_axis, swap)
        acc = pair_join(acc, got, second)
    group = block.shape[0]
    size = lax.axis_size(rows_axes)
    table = [block]
    for m in range(1, BAND // group + 1):
        table = [shifted(block, rows_axes, size, -m * group)] + table
        table.append(shifted(block, rows_axes, size, m * group))
    return jnp.concatenate(table), acc


def band_products(table, tiles, index, mask):
    picked = jnp.take(table, index, axis=0)
    picked = jnp.where(mask[:, None, None], picked, jnp.zeros((), picked.dtype))
    return jnp.einsum("sfk,srk->fr", picked, tiles, preferred_element_type=jnp.float32)


def per_device(
    features, weight_matrix, bias_vector, adjacency_tiles, tile_cols, tile_count, out_grad
):
    feature_width, rows_here = features.shape
    rows_count = lax.axis_size(ROWS)
    cols_count = lax.axis_size("cols")
    assert adjacency_tiles.shape[0] == 1
    assert rows_count & (rows_count - 1) == 0 and rows_count >= 64
    assert cols_count & (cols_count - 1) == 0
    row = lax.axis_index(ROWS)
    col = lax.axis_index("cols")
    tiles = adjacency_tiles[0]
    column_ids = tile_cols[0]
    count = tile_count[0]
    slot_count = column_ids.shape[0]
    group = 8

    alive = jnp.arange(slot_count, dtype=jnp.int32) < count
    offset = (column_ids - row + rows_count // 2) % rows_count - rows_count // 2
    near = jnp.abs(offset) <= BAND
    is_hub = count == slot_count
    near_mask = alive & near
    far = alive & jnp.logical_not(near) & jnp.logical_not(is_hub)
    has_far = jnp.any(far)
    index = jnp.where(near, offset + row % group + BAND, BAND)
    far_slot = jnp.argmax(far)
    far_tile = lax.dynamic_index_in_dim(tiles, far_slot, 0, keepdims=False)
    far_tile = jnp.where(has_far, far_tile, jnp.zeros((), far_tile.dtype))

    def hub_terms(x):
        own = jnp.where(is_hub, x, jnp.zeros((), x.dtype)).astype(jnp.float32)
        back = jnp.einsum("fk,kr->fr", x, far_tile, preferred_element_type=jnp.float32)
        return own, back

    def finish(table, hub_panel, hub_sum):
        total = band_products(table, tiles, index, near_mask)
        total = total + jnp.einsum(
            "fk,rk->fr", hub_panel, far_tile, preferred_element_type=jnp.float32
        )
        return total + jnp.where(is_hub, hub_sum, jnp.zeros((), hub_sum.dtype))

    own, back = hub_terms(features)
    table, reduced = exchange(features, jnp.concatenate([own, back]), ROWS, CARRY)
    hub_panel = reduced[:feature_width].astype(jnp.bfloat16)
    aggregated = finish(table, hub_panel, reduced[feature_width:]).astype(jnp.bfloat16)

    both = gather_axis(jnp.stack([aggregated, out_grad]), "cols")
    both = jnp.swapaxes(both, 0, 1)
    agg_full = both[0].reshape(-1, rows_here)
    grad_full = both[1].reshape(-1, rows_here)

    preact = (
        jnp.dot(weight_matrix, agg_full, preferred_element_type=jnp.float32)
        + bias_vector[:, None]
    )
    sigmoid_pre = jax.nn.sigmoid(preact)
    pre_grad = (
        grad_full.astype(jnp.float32) * sigmoid_pre * (1.0 + preact * (1.0 - sigmoid_pre))
    ).astype(jnp.bfloat16)
    start = col * feature_width
    own_pre = lax.dynamic_slice_in_dim(preact, start, feature_width, 0)
    own_sig = lax.dynamic_slice_in_dim(sigmoid_pre, start, feature_width, 0)
    layer_out = (own_pre * own_sig).astype(jnp.bfloat16)
    own_grad = lax.dynamic_slice_in_dim(pre_grad, start, feature_width, 0)
    weight_cols = lax.dynamic_slice_in_dim(weight_matrix, start, feature_width, 1)
    agg_grad = jnp.einsum(
        "oi,on->in", weight_cols, pre_grad, preferred_element_type=jnp.float32
    ).astype(jnp.bfloat16)
    weight_part = jnp.einsum(
        "fn,in->fi", own_grad, agg_full, preferred_element_type=jnp.float32
    )
    bias_part = jnp.sum(own_grad.astype(jnp.float32), axis=1)

    own2, back2 = hub_terms(agg_grad)
    width = weight_part.shape[1]
    lanes = rows_here
    bias_rows = jnp.zeros((8, lanes), jnp.float32).at[0, :feature_width].set(bias_part)
    spare = jnp.zeros((8, lanes), jnp.float32)
    packed = jnp.concatenate(
        [own2, back2, spare, weight_part.reshape(-1, lanes), bias_rows]
    )
    table2, reduced2 = exchange(agg_grad, packed, ROWS, CARRY, split=True)
    hub_panel2 = reduced2[:feature_width].astype(jnp.bfloat16)
    hub_sum2 = reduced2[feature_width : 2 * feature_width]
    feature_grad = finish(table2, hub_panel2, hub_sum2).astype(jnp.bfloat16)
    grad_scale = 1.0 / math.sqrt(rows_here * rows_count)
    weight_rows = feature_width * width // lanes
    first = 2 * feature_width + 8
    weight_grad = (
        reduced2[first : first + weight_rows].reshape(feature_width, width) * grad_scale
    )
    bias_grad = reduced2[first + weight_rows, :feature_width] * grad_scale
    return (layer_out, feature_grad, weight_grad, bias_grad)


ROWS = ("zh", "zl", "y", "core")
CARRY = ("y", "core")


def solution(mesh):
    rows_count = mesh.shape["rows"]
    cols_count = mesh.shape["cols"]
    assert rows_count % 32 == 0
    split = jax.sharding.Mesh(
        mesh.devices.reshape(rows_count // 32, 4, 4, 2, cols_count), ROWS + ("cols",)
    )
    return jax.shard_map(
        per_device,
        mesh=split,
        in_specs=(
            P("cols", ROWS),
            P(),
            P(),
            P(ROWS, None, None, None),
            P(ROWS, None),
            P(ROWS),
            P("cols", ROWS),
        ),
        out_specs=(P("cols", ROWS), P("cols", ROWS), P("cols", None), P("cols")),
        check_vma=False,
    )
```

```python
import math

import jax
import jax.numpy as jnp
from jax import lax
from jax.sharding import PartitionSpec as P

BAND = 16
GROUP_ROUNDS = 2


def shifted(x, axis, size, d):
    return lax.ppermute(x, axis, [((i + d) % size, i) for i in range(size)])


def pair_join(mine, got, upper):
    return jnp.where(upper, jnp.concatenate([got, mine]), jnp.concatenate([mine, got]))


def gather_axis(x, axis):
    size = lax.axis_size(axis)
    spread = jnp.broadcast_to(x[None], (size,) + x.shape)
    return lax.all_to_all(spread, axis, 0, 0, tiled=True)


def exchange(panel, acc, rows_axes, carry_axes, split=False):
    lanes = panel.shape[-1]
    block = panel[None]
    axes = list(reversed(rows_axes))
    if split:
        core_axis = axes.pop(0)
        second = lax.axis_index(core_axis) == 1
        swap = [(0, 1), (1, 0)]
        half = acc.shape[0] // 2
        mine = jnp.where(second, acc[half:], acc[:half])
        other = jnp.where(second, acc[:half], acc[half:])
        flat = block.reshape(-1, lanes).astype(jnp.float32)
        got = lax.ppermute(jnp.concatenate([flat, other]), core_axis, swap)
        got_block = got[: flat.shape[0]].reshape(block.shape).astype(block.dtype)
        block = pair_join(block, got_block, second)
        acc = mine + got[flat.shape[0] :]
    for axis in axes:
        carry = axis in carry_axes
        if carry:
            flat = block.reshape(-1, lanes).astype(jnp.float32)
            send = jnp.concatenate([flat, acc])
        else:
            send = acc
        got = gather_axis(send, axis)
        if carry:
            rows_in = flat.shape[0]
            block = got[:, :rows_in].reshape((-1,) + block.shape[1:]).astype(block.dtype)
            parts = got[:, rows_in:]
        else:
            parts = got
        acc = parts[0]
        for d in range(1, parts.shape[0]):
            acc = acc + parts[d]
    if split:
        got = lax.ppermute(acc, core_axis, swap)
        acc = pair_join(acc, got, second)
    group = block.shape[0]
    size = lax.axis_size(rows_axes)
    pair = lax.axis_size(rows_axes[-1])
    assert BAND == 2 * group and pair == 2
    upper_core = lax.axis_index(rows_axes[-1]) == 1

    def one_side(m):
        shifts = [-m * group if i % pair == 0 else m * group for i in range(size)]
        return lax.ppermute(block, rows_axes, [((i + s) % size, i) for i, s in enumerate(shifts)])

    fetched = jnp.stack([one_side(2), one_side(1)])
    other = lax.ppermute(fetched, rows_axes[-1], [(0, 1), (1, 0)])
    below = jnp.where(upper_core, other, fetched)
    above = jnp.where(upper_core, fetched, other)
    table = [below[0], below[1], block, above[1], above[0]]
    return jnp.concatenate(table), acc


def band_products(table, tiles, index, mask):
    picked = jnp.take(table, index, axis=0)
    picked = jnp.where(mask[:, None, None], picked, jnp.zeros((), picked.dtype))
    return jnp.einsum("sfk,srk->fr", picked, tiles, preferred_element_type=jnp.float32)


def per_device(
    features, weight_matrix, bias_vector, adjacency_tiles, tile_cols, tile_count, out_grad
):
    feature_width, rows_here = features.shape
    rows_count = lax.axis_size(ROWS)
    cols_count = lax.axis_size("cols")
    assert adjacency_tiles.shape[0] == 1
    assert rows_count & (rows_count - 1) == 0 and rows_count >= 64
    assert cols_count & (cols_count - 1) == 0
    row = lax.axis_index(ROWS)
    col = lax.axis_index("cols")
    tiles = adjacency_tiles[0]
    column_ids = tile_cols[0]
    count = tile_count[0]
    slot_count = column_ids.shape[0]
    group = 8

    alive = jnp.arange(slot_count, dtype=jnp.int32) < count
    offset = (column_ids - row + rows_count // 2) % rows_count - rows_count // 2
    near = jnp.abs(offset) <= BAND
    is_hub = count == slot_count
    near_mask = alive & near
    far = alive & jnp.logical_not(near) & jnp.logical_not(is_hub)
    has_far = jnp.any(far)
    index = jnp.where(near, offset + row % group + BAND, BAND)
    far_slot = jnp.argmax(far)
    far_tile = lax.dynamic_index_in_dim(tiles, far_slot, 0, keepdims=False)
    far_tile = jnp.where(has_far, far_tile, jnp.zeros((), far_tile.dtype))

    def hub_terms(x):
        own = jnp.where(is_hub, x, jnp.zeros((), x.dtype)).astype(jnp.float32)
        back = jnp.einsum("fk,kr->fr", x, far_tile, preferred_element_type=jnp.float32)
        return own, back

    def finish(table, hub_panel, hub_sum):
        total = band_products(table, tiles, index, near_mask)
        total = total + jnp.einsum(
            "fk,rk->fr", hub_panel, far_tile, preferred_element_type=jnp.float32
        )
        return total + jnp.where(is_hub, hub_sum, jnp.zeros((), hub_sum.dtype))

    own, back = hub_terms(features)
    table, reduced = exchange(features, jnp.concatenate([own, back]), ROWS, CARRY)
    hub_panel = reduced[:feature_width].astype(jnp.bfloat16)
    aggregated = finish(table, hub_panel, reduced[feature_width:]).astype(jnp.bfloat16)

    both = gather_axis(jnp.stack([aggregated, out_grad]), "cols")
    both = jnp.swapaxes(both, 0, 1)
    agg_full = both[0].reshape(-1, rows_here)
    grad_full = both[1].reshape(-1, rows_here)

    preact = (
        jnp.dot(weight_matrix, agg_full, preferred_element_type=jnp.float32)
        + bias_vector[:, None]
    )
    sigmoid_pre = jax.nn.sigmoid(preact)
    pre_grad = (
        grad_full.astype(jnp.float32) * sigmoid_pre * (1.0 + preact * (1.0 - sigmoid_pre))
    ).astype(jnp.bfloat16)
    start = col * feature_width
    own_pre = lax.dynamic_slice_in_dim(preact, start, feature_width, 0)
    own_sig = lax.dynamic_slice_in_dim(sigmoid_pre, start, feature_width, 0)
    layer_out = (own_pre * own_sig).astype(jnp.bfloat16)
    own_grad = lax.dynamic_slice_in_dim(pre_grad, start, feature_width, 0)
    weight_cols = lax.dynamic_slice_in_dim(weight_matrix, start, feature_width, 1)
    agg_grad = jnp.einsum(
        "oi,on->in", weight_cols, pre_grad, preferred_element_type=jnp.float32
    ).astype(jnp.bfloat16)
    weight_part = jnp.einsum(
        "fn,in->fi", own_grad, agg_full, preferred_element_type=jnp.float32
    )
    bias_part = jnp.sum(own_grad.astype(jnp.float32), axis=1)

    own2, back2 = hub_terms(agg_grad)
    width = weight_part.shape[1]
    lanes = rows_here
    bias_rows = jnp.zeros((8, lanes), jnp.float32).at[0, :feature_width].set(bias_part)
    spare = jnp.zeros((8, lanes), jnp.float32)
    packed = jnp.concatenate(
        [own2, back2, spare, weight_part.reshape(-1, lanes), bias_rows]
    )
    table2, reduced2 = exchange(agg_grad, packed, ROWS, CARRY, split=True)
    hub_panel2 = reduced2[:feature_width].astype(jnp.bfloat16)
    hub_sum2 = reduced2[feature_width : 2 * feature_width]
    feature_grad = finish(table2, hub_panel2, hub_sum2).astype(jnp.bfloat16)
    grad_scale = 1.0 / math.sqrt(rows_here * rows_count)
    weight_rows = feature_width * width // lanes
    first = 2 * feature_width + 8
    weight_grad = (
        reduced2[first : first + weight_rows].reshape(feature_width, width) * grad_scale
    )
    bias_grad = reduced2[first + weight_rows, :feature_width] * grad_scale
    return (layer_out, feature_grad, weight_grad, bias_grad)


ROWS = ("zh", "zl", "y", "core")
CARRY = ("y", "core")


def solution(mesh):
    rows_count = mesh.shape["rows"]
    cols_count = mesh.shape["cols"]
    assert rows_count % 32 == 0
    split = jax.sharding.Mesh(
        mesh.devices.reshape(rows_count // 32, 4, 4, 2, cols_count), ROWS + ("cols",)
    )
    return jax.shard_map(
        per_device,
        mesh=split,
        in_specs=(
            P("cols", ROWS),
            P(),
            P(),
            P(ROWS, None, None, None),
            P(ROWS, None),
            P(ROWS),
            P("cols", ROWS),
        ),
        out_specs=(P("cols", ROWS), P("cols", ROWS), P("cols", None), P("cols")),
        check_vma=False,
    )
```

```python
import math

import jax
import jax.numpy as jnp
from jax import lax
from jax.sharding import PartitionSpec as P

BAND = 16
GROUP_ROUNDS = 2


def shifted(x, axis, size, d):
    return lax.ppermute(x, axis, [((i + d) % size, i) for i in range(size)])


def pair_join(mine, got, upper):
    return jnp.where(upper, jnp.concatenate([got, mine]), jnp.concatenate([mine, got]))


def gather_axis(x, axis):
    size = lax.axis_size(axis)
    spread = jnp.broadcast_to(x[None], (size,) + x.shape)
    return lax.all_to_all(spread, axis, 0, 0, tiled=True)


def exchange(panel, acc, rows_axes, carry_axes, split=False):
    lanes = panel.shape[-1]
    block = panel[None]
    axes = list(reversed(rows_axes))
    if split:
        core_axis = axes.pop(0)
        second = lax.axis_index(core_axis) == 1
        swap = [(0, 1), (1, 0)]
        half = acc.shape[0] // 2
        mine = jnp.where(second, acc[half:], acc[:half])
        other = jnp.where(second, acc[:half], acc[half:])
        flat = block.reshape(-1, lanes).astype(jnp.float32)
        got = lax.ppermute(jnp.concatenate([flat, other]), core_axis, swap)
        got_block = got[: flat.shape[0]].reshape(block.shape).astype(block.dtype)
        block = pair_join(block, got_block, second)
        acc = mine + got[flat.shape[0] :]
    for axis in axes:
        carry = axis in carry_axes
        if carry:
            flat = block.reshape(-1, lanes).astype(jnp.float32)
            send = jnp.concatenate([flat, acc])
        else:
            send = acc
        got = gather_axis(send, axis)
        if carry:
            rows_in = flat.shape[0]
            block = got[:, :rows_in].reshape((-1,) + block.shape[1:]).astype(block.dtype)
            parts = got[:, rows_in:]
        else:
            parts = got
        acc = parts[0]
        for d in range(1, parts.shape[0]):
            acc = acc + parts[d]
    if split:
        got = lax.ppermute(acc, core_axis, swap)
        acc = pair_join(acc, got, second)
    group = block.shape[0]
    size = lax.axis_size(rows_axes)
    table = [block]
    for m in range(1, BAND // group + 1):
        table = [shifted(block, rows_axes, size, -m * group)] + table
        table.append(shifted(block, rows_axes, size, m * group))
    return jnp.concatenate(table), acc


def band_products(table, tiles, index, mask):
    picked = jnp.take(table, index, axis=0)
    picked = jnp.where(mask[:, None, None], picked, jnp.zeros((), picked.dtype))
    return jnp.einsum("sfk,srk->fr", picked, tiles, preferred_element_type=jnp.float32)


def per_device(
    features, weight_matrix, bias_vector, adjacency_tiles, tile_cols, tile_count, out_grad
):
    feature_width, rows_here = features.shape
    rows_count = lax.axis_size(ROWS)
    cols_count = lax.axis_size("cols")
    assert adjacency_tiles.shape[0] == 1
    assert rows_count & (rows_count - 1) == 0 and rows_count >= 64
    assert cols_count & (cols_count - 1) == 0
    row = lax.axis_index(ROWS)
    col = lax.axis_index("cols")
    tiles = adjacency_tiles[0]
    column_ids = tile_cols[0]
    count = tile_count[0]
    slot_count = column_ids.shape[0]
    group = 8

    alive = jnp.arange(slot_count, dtype=jnp.int32) < count
    offset = (column_ids - row + rows_count // 2) % rows_count - rows_count // 2
    near = jnp.abs(offset) <= BAND
    is_hub = count == slot_count
    near_mask = alive & near
    far = alive & jnp.logical_not(near) & jnp.logical_not(is_hub)
    has_far = jnp.any(far)
    index = jnp.where(near, offset + row % group + BAND, BAND)
    far_slot = jnp.argmax(far)
    far_tile = lax.dynamic_index_in_dim(tiles, far_slot, 0, keepdims=False)
    far_tile = jnp.where(has_far, far_tile, jnp.zeros((), far_tile.dtype))

    def hub_terms(x):
        own = jnp.where(is_hub, x, jnp.zeros((), x.dtype)).astype(jnp.float32)
        back = jnp.einsum("fk,kr->fr", x, far_tile, preferred_element_type=jnp.float32)
        return own, back

    def finish(table, hub_panel, hub_sum):
        total = band_products(table, tiles, index, near_mask)
        total = total + jnp.einsum(
            "fk,rk->fr", hub_panel, far_tile, preferred_element_type=jnp.float32
        )
        return total + jnp.where(is_hub, hub_sum, jnp.zeros((), hub_sum.dtype))

    own, back = hub_terms(features)
    table, reduced = exchange(features, jnp.concatenate([own, back]), ROWS, CARRY, split=True)
    hub_panel = reduced[:feature_width].astype(jnp.bfloat16)
    aggregated = finish(table, hub_panel, reduced[feature_width:]).astype(jnp.bfloat16)

    both = gather_axis(jnp.stack([aggregated, out_grad]), "cols")
    both = jnp.swapaxes(both, 0, 1)
    agg_full = both[0].reshape(-1, rows_here)
    grad_full = both[1].reshape(-1, rows_here)

    preact = (
        jnp.dot(weight_matrix, agg_full, preferred_element_type=jnp.float32)
        + bias_vector[:, None]
    )
    sigmoid_pre = jax.nn.sigmoid(preact)
    pre_grad = (
        grad_full.astype(jnp.float32) * sigmoid_pre * (1.0 + preact * (1.0 - sigmoid_pre))
    ).astype(jnp.bfloat16)
    start = col * feature_width
    own_pre = lax.dynamic_slice_in_dim(preact, start, feature_width, 0)
    own_sig = lax.dynamic_slice_in_dim(sigmoid_pre, start, feature_width, 0)
    layer_out = (own_pre * own_sig).astype(jnp.bfloat16)
    own_grad = lax.dynamic_slice_in_dim(pre_grad, start, feature_width, 0)
    weight_cols = lax.dynamic_slice_in_dim(weight_matrix, start, feature_width, 1)
    agg_grad = jnp.einsum(
        "oi,on->in", weight_cols, pre_grad, preferred_element_type=jnp.float32
    ).astype(jnp.bfloat16)
    weight_part = jnp.einsum(
        "fn,in->fi", own_grad, agg_full, preferred_element_type=jnp.float32
    )
    bias_part = jnp.sum(own_grad.astype(jnp.float32), axis=1)

    own2, back2 = hub_terms(agg_grad)
    width = weight_part.shape[1]
    lanes = rows_here
    bias_rows = jnp.zeros((8, lanes), jnp.float32).at[0, :feature_width].set(bias_part)
    spare = jnp.zeros((8, lanes), jnp.float32)
    packed = jnp.concatenate(
        [own2, back2, spare, weight_part.reshape(-1, lanes), bias_rows]
    )
    table2, reduced2 = exchange(agg_grad, packed, ROWS, CARRY, split=True)
    hub_panel2 = reduced2[:feature_width].astype(jnp.bfloat16)
    hub_sum2 = reduced2[feature_width : 2 * feature_width]
    feature_grad = finish(table2, hub_panel2, hub_sum2).astype(jnp.bfloat16)
    grad_scale = 1.0 / math.sqrt(rows_here * rows_count)
    weight_rows = feature_width * width // lanes
    first = 2 * feature_width + 8
    weight_grad = (
        reduced2[first : first + weight_rows].reshape(feature_width, width) * grad_scale
    )
    bias_grad = reduced2[first + weight_rows, :feature_width] * grad_scale
    return (layer_out, feature_grad, weight_grad, bias_grad)


ROWS = ("zh", "zl", "y", "core")
CARRY = ("y", "core")


def solution(mesh):
    rows_count = mesh.shape["rows"]
    cols_count = mesh.shape["cols"]
    assert rows_count % 32 == 0
    split = jax.sharding.Mesh(
        mesh.devices.reshape(rows_count // 32, 4, 4, 2, cols_count), ROWS + ("cols",)
    )
    return jax.shard_map(
        per_device,
        mesh=split,
        in_specs=(
            P("cols", ROWS),
            P(),
            P(),
            P(ROWS, None, None, None),
            P(ROWS, None),
            P(ROWS),
            P("cols", ROWS),
        ),
        out_specs=(P("cols", ROWS), P("cols", ROWS), P("cols", None), P("cols")),
        check_vma=False,
    )
```

```python
import math

import jax
import jax.numpy as jnp
from jax import lax
from jax.sharding import PartitionSpec as P


BAND = 16


def shifted(x, axis, size, d):
    return lax.ppermute(x, axis, [((i + d) % size, i) for i in range(size)])


def pair_join(mine, got, upper):
    return jnp.where(upper, jnp.concatenate([got, mine]), jnp.concatenate([mine, got]))


def gather_axis(x, axis):
    size = lax.axis_size(axis)
    spread = jnp.broadcast_to(x[None], (size,) + x.shape)
    return lax.all_to_all(spread, axis, 0, 0, tiled=True)


def exchange(panel, acc, rows_axes, carry_axes, split=False):
    lanes = panel.shape[-1]
    block = panel[None]
    axes = list(reversed(rows_axes))
    if split:
        core_axis = axes.pop(0)
        second = lax.axis_index(core_axis) == 1
        swap = [(0, 1), (1, 0)]
        half = acc.shape[0] // 2
        mine = jnp.where(second, acc[half:], acc[:half])
        other = jnp.where(second, acc[:half], acc[half:])
        flat = block.reshape(-1, lanes).astype(jnp.float32)
        got = lax.ppermute(jnp.concatenate([flat, other]), core_axis, swap)
        got_block = got[: flat.shape[0]].reshape(block.shape).astype(block.dtype)
        block = pair_join(block, got_block, second)
        acc = mine + got[flat.shape[0] :]
    for axis in axes:
        carry = axis in carry_axes
        if carry:
            flat = block.reshape(-1, lanes).astype(jnp.float32)
            send = jnp.concatenate([flat, acc])
        else:
            send = acc
        got = gather_axis(send, axis)
        if carry:
            rows_in = flat.shape[0]
            block = got[:, :rows_in].reshape((-1,) + block.shape[1:]).astype(block.dtype)
            parts = got[:, rows_in:]
        else:
            parts = got
        acc = parts[0]
        for d in range(1, parts.shape[0]):
            acc = acc + parts[d]
    if split:
        got = lax.ppermute(acc, core_axis, swap)
        acc = pair_join(acc, got, second)
    group = block.shape[0]
    size = lax.axis_size(rows_axes)
    table = [block]
    for m in range(1, BAND // group + 1):
        table = [shifted(block, rows_axes, size, -m * group)] + table
        table.append(shifted(block, rows_axes, size, m * group))
    return jnp.concatenate(table), acc


def band_products(table, tiles, index, mask):
    picked = jnp.take(table, index, axis=0)
    picked = jnp.where(mask[:, None, None], picked, jnp.zeros((), picked.dtype))
    return jnp.einsum("sfk,srk->fr", picked, tiles, preferred_element_type=jnp.float32)


def per_device(
    features, weight_matrix, bias_vector, adjacency_tiles, tile_cols, tile_count, out_grad
):
    feature_width, rows_here = features.shape
    rows_count = lax.axis_size(ROWS)
    cols_count = lax.axis_size("cols")
    assert adjacency_tiles.shape[0] == 1
    assert rows_count & (rows_count - 1) == 0 and rows_count >= 64
    assert cols_count & (cols_count - 1) == 0
    row = lax.axis_index(ROWS)
    col = lax.axis_index("cols")
    tiles = adjacency_tiles[0]
    column_ids = tile_cols[0]
    count = tile_count[0]
    slot_count = column_ids.shape[0]
    group = 8

    alive = jnp.arange(slot_count, dtype=jnp.int32) < count
    offset = (column_ids - row + rows_count // 2) % rows_count - rows_count // 2
    near = jnp.abs(offset) <= BAND
    is_hub = count == slot_count
    near_mask = alive & near
    far = alive & jnp.logical_not(near) & jnp.logical_not(is_hub)
    has_far = jnp.any(far)
    index = jnp.where(near, offset + row % group + BAND, BAND)
    far_slot = jnp.argmax(far)
    far_tile = lax.dynamic_index_in_dim(tiles, far_slot, 0, keepdims=False)
    far_tile = jnp.where(has_far, far_tile, jnp.zeros((), far_tile.dtype))

    def hub_terms(x):
        own = jnp.where(is_hub, x, jnp.zeros((), x.dtype)).astype(jnp.float32)
        back = jnp.einsum("fk,kr->fr", x, far_tile, preferred_element_type=jnp.float32)
        return own, back

    def finish(table, hub_panel, hub_sum):
        total = band_products(table, tiles, index, near_mask)
        total = total + jnp.einsum(
            "fk,rk->fr", hub_panel, far_tile, preferred_element_type=jnp.float32
        )
        return total + jnp.where(is_hub, hub_sum, jnp.zeros((), hub_sum.dtype))

    own, back = hub_terms(features)
    table, reduced = exchange(
        features, jnp.concatenate([own, back]), ROWS, CARRY, split=True
    )
    hub_panel = reduced[:feature_width].astype(jnp.bfloat16)
    aggregated = finish(table, hub_panel, reduced[feature_width:]).astype(jnp.bfloat16)

    both = gather_axis(jnp.stack([aggregated, out_grad]), "cols")
    both = jnp.swapaxes(both, 0, 1)
    agg_full = both[0].reshape(-1, rows_here)
    grad_full = both[1].reshape(-1, rows_here)

    preact = (
        jnp.dot(weight_matrix, agg_full, preferred_element_type=jnp.float32)
        + bias_vector[:, None]
    )
    sigmoid_pre = jax.nn.sigmoid(preact)
    pre_grad = (
        grad_full.astype(jnp.float32) * sigmoid_pre * (1.0 + preact * (1.0 - sigmoid_pre))
    ).astype(jnp.bfloat16)
    start = col * feature_width
    own_pre = lax.dynamic_slice_in_dim(preact, start, feature_width, 0)
    own_sig = lax.dynamic_slice_in_dim(sigmoid_pre, start, feature_width, 0)
    layer_out = (own_pre * own_sig).astype(jnp.bfloat16)
    own_grad = lax.dynamic_slice_in_dim(pre_grad, start, feature_width, 0)
    weight_cols = lax.dynamic_slice_in_dim(weight_matrix, start, feature_width, 1)
    agg_grad = jnp.einsum(
        "oi,on->in", weight_cols, pre_grad, preferred_element_type=jnp.float32
    ).astype(jnp.bfloat16)
    weight_part = jnp.einsum(
        "fn,in->fi", own_grad, agg_full, preferred_element_type=jnp.float32
    )
    bias_part = jnp.sum(own_grad.astype(jnp.float32), axis=1)

    own2, back2 = hub_terms(agg_grad)
    width = weight_part.shape[1]
    lanes = rows_here
    bias_rows = jnp.zeros((8, lanes), jnp.float32).at[0, :feature_width].set(bias_part)
    spare = jnp.zeros((8, lanes), jnp.float32)
    packed = jnp.concatenate(
        [own2, back2, spare, weight_part.reshape(-1, lanes), bias_rows]
    )
    table2, reduced2 = exchange(agg_grad, packed, ROWS, CARRY, split=True)
    hub_panel2 = reduced2[:feature_width].astype(jnp.bfloat16)
    hub_sum2 = reduced2[feature_width : 2 * feature_width]
    feature_grad = finish(table2, hub_panel2, hub_sum2).astype(jnp.bfloat16)
    grad_scale = 1.0 / math.sqrt(rows_here * rows_count)
    weight_rows = feature_width * width // lanes
    first = 2 * feature_width + 8
    weight_grad = (
        reduced2[first : first + weight_rows].reshape(feature_width, width) * grad_scale
    )
    bias_grad = reduced2[first + weight_rows, :feature_width] * grad_scale
    return (layer_out, feature_grad, weight_grad, bias_grad)


ROWS = ("zh", "zl", "y", "core")
CARRY = ("y", "core")


def solution(mesh):
    rows_count = mesh.shape["rows"]
    cols_count = mesh.shape["cols"]
    assert rows_count % 32 == 0
    split = jax.sharding.Mesh(
        mesh.devices.reshape(rows_count // 32, 4, 4, 2, cols_count), ROWS + ("cols",)
    )
    return jax.shard_map(
        per_device,
        mesh=split,
        in_specs=(
            P("cols", ROWS),
            P(),
            P(),
            P(ROWS, None, None, None),
            P(ROWS, None),
            P(ROWS),
            P("cols", ROWS),
        ),
        out_specs=(P("cols", ROWS), P("cols", ROWS), P("cols", None), P("cols")),
        check_vma=False,
    )
```

```python
import math

import jax
import jax.numpy as jnp
from jax import lax
from jax.sharding import PartitionSpec as P

BAND = 16
GROUP_ROUNDS = 2


def shifted(x, axis, size, d):
    return lax.ppermute(x, axis, [((i + d) % size, i) for i in range(size)])


def pair_join(mine, got, upper):
    return jnp.where(upper, jnp.concatenate([got, mine]), jnp.concatenate([mine, got]))


def gather_axis(x, axis):
    size = lax.axis_size(axis)
    spread = jnp.broadcast_to(x[None], (size,) + x.shape)
    return lax.all_to_all(spread, axis, 0, 0, tiled=True)


def exchange(panel, acc, rows_axes, carry_axes, split=False):
    lanes = panel.shape[-1]
    block = panel[None]
    axes = list(reversed(rows_axes))
    if split:
        core_axis = axes.pop(0)
        second = lax.axis_index(core_axis) == 1
        swap = [(0, 1), (1, 0)]
        half = acc.shape[0] // 2
        mine = jnp.where(second, acc[half:], acc[:half])
        other = jnp.where(second, acc[:half], acc[half:])
        flat = block.reshape(-1, lanes).astype(jnp.float32)
        got = lax.ppermute(jnp.concatenate([flat, other]), core_axis, swap)
        got_block = got[: flat.shape[0]].reshape(block.shape).astype(block.dtype)
        block = pair_join(block, got_block, second)
        acc = mine + got[flat.shape[0] :]
    if axes[-2:] == ["zl", "zh"]:
        axes[-2:] = ["zh", "zl"]
    for axis in axes:
        carry = axis in carry_axes
        if carry:
            flat = block.reshape(-1, lanes).astype(jnp.float32)
            send = jnp.concatenate([flat, acc])
        else:
            send = acc
        got = gather_axis(send, axis)
        if carry:
            rows_in = flat.shape[0]
            block = got[:, :rows_in].reshape((-1,) + block.shape[1:]).astype(block.dtype)
            parts = got[:, rows_in:]
        else:
            parts = got
        acc = parts[0]
        for d in range(1, parts.shape[0]):
            acc = acc + parts[d]
    if split:
        got = lax.ppermute(acc, core_axis, swap)
        acc = pair_join(acc, got, second)
    group = block.shape[0]
    size = lax.axis_size(rows_axes)
    table = [block]
    for m in range(1, BAND // group + 1):
        table = [shifted(block, rows_axes, size, -m * group)] + table
        table.append(shifted(block, rows_axes, size, m * group))
    return jnp.concatenate(table), acc


def band_products(table, tiles, index, mask):
    picked = jnp.take(table, index, axis=0)
    picked = jnp.where(mask[:, None, None], picked, jnp.zeros((), picked.dtype))
    return jnp.einsum("sfk,srk->fr", picked, tiles, preferred_element_type=jnp.float32)


def per_device(
    features, weight_matrix, bias_vector, adjacency_tiles, tile_cols, tile_count, out_grad
):
    feature_width, rows_here = features.shape
    rows_count = lax.axis_size(ROWS)
    cols_count = lax.axis_size("cols")
    assert adjacency_tiles.shape[0] == 1
    assert rows_count & (rows_count - 1) == 0 and rows_count >= 64
    assert cols_count & (cols_count - 1) == 0
    row = lax.axis_index(ROWS)
    col = lax.axis_index("cols")
    tiles = adjacency_tiles[0]
    column_ids = tile_cols[0]
    count = tile_count[0]
    slot_count = column_ids.shape[0]
    group = 8

    alive = jnp.arange(slot_count, dtype=jnp.int32) < count
    offset = (column_ids - row + rows_count // 2) % rows_count - rows_count // 2
    near = jnp.abs(offset) <= BAND
    is_hub = count == slot_count
    near_mask = alive & near
    far = alive & jnp.logical_not(near) & jnp.logical_not(is_hub)
    has_far = jnp.any(far)
    index = jnp.where(near, offset + row % group + BAND, BAND)
    far_slot = jnp.argmax(far)
    far_tile = lax.dynamic_index_in_dim(tiles, far_slot, 0, keepdims=False)
    far_tile = jnp.where(has_far, far_tile, jnp.zeros((), far_tile.dtype))

    def hub_terms(x):
        own = jnp.where(is_hub, x, jnp.zeros((), x.dtype)).astype(jnp.float32)
        back = jnp.einsum("fk,kr->fr", x, far_tile, preferred_element_type=jnp.float32)
        return own, back

    def finish(table, hub_panel, hub_sum):
        total = band_products(table, tiles, index, near_mask)
        total = total + jnp.einsum(
            "fk,rk->fr", hub_panel, far_tile, preferred_element_type=jnp.float32
        )
        return total + jnp.where(is_hub, hub_sum, jnp.zeros((), hub_sum.dtype))

    own, back = hub_terms(features)
    table, reduced = exchange(features, jnp.concatenate([own, back]), ROWS, CARRY, split=True)
    hub_panel = reduced[:feature_width].astype(jnp.bfloat16)
    aggregated = finish(table, hub_panel, reduced[feature_width:]).astype(jnp.bfloat16)

    both = gather_axis(jnp.stack([aggregated, out_grad]), "cols")
    both = jnp.swapaxes(both, 0, 1)
    agg_full = both[0].reshape(-1, rows_here)
    grad_full = both[1].reshape(-1, rows_here)

    preact = (
        jnp.dot(weight_matrix, agg_full, preferred_element_type=jnp.float32)
        + bias_vector[:, None]
    )
    sigmoid_pre = jax.nn.sigmoid(preact)
    pre_grad = (
        grad_full.astype(jnp.float32) * sigmoid_pre * (1.0 + preact * (1.0 - sigmoid_pre))
    ).astype(jnp.bfloat16)
    start = col * feature_width
    own_pre = lax.dynamic_slice_in_dim(preact, start, feature_width, 0)
    own_sig = lax.dynamic_slice_in_dim(sigmoid_pre, start, feature_width, 0)
    layer_out = (own_pre * own_sig).astype(jnp.bfloat16)
    own_grad = lax.dynamic_slice_in_dim(pre_grad, start, feature_width, 0)
    weight_cols = lax.dynamic_slice_in_dim(weight_matrix, start, feature_width, 1)
    agg_grad = jnp.einsum(
        "oi,on->in", weight_cols, pre_grad, preferred_element_type=jnp.float32
    ).astype(jnp.bfloat16)
    weight_part = jnp.einsum(
        "fn,in->fi", own_grad, agg_full, preferred_element_type=jnp.float32
    )
    bias_part = jnp.sum(own_grad.astype(jnp.float32), axis=1)

    own2, back2 = hub_terms(agg_grad)
    width = weight_part.shape[1]
    lanes = rows_here
    bias_rows = jnp.zeros((8, lanes), jnp.float32).at[0, :feature_width].set(bias_part)
    spare = jnp.zeros((8, lanes), jnp.float32)
    packed = jnp.concatenate(
        [own2, back2, spare, weight_part.reshape(-1, lanes), bias_rows]
    )
    table2, reduced2 = exchange(agg_grad, packed, ROWS, CARRY, split=True)
    hub_panel2 = reduced2[:feature_width].astype(jnp.bfloat16)
    hub_sum2 = reduced2[feature_width : 2 * feature_width]
    feature_grad = finish(table2, hub_panel2, hub_sum2).astype(jnp.bfloat16)
    grad_scale = 1.0 / math.sqrt(rows_here * rows_count)
    weight_rows = feature_width * width // lanes
    first = 2 * feature_width + 8
    weight_grad = (
        reduced2[first : first + weight_rows].reshape(feature_width, width) * grad_scale
    )
    bias_grad = reduced2[first + weight_rows, :feature_width] * grad_scale
    return (layer_out, feature_grad, weight_grad, bias_grad)


ROWS = ("zh", "zl", "y", "core")
CARRY = ("y", "core")


def solution(mesh):
    rows_count = mesh.shape["rows"]
    cols_count = mesh.shape["cols"]
    assert rows_count % 32 == 0
    split = jax.sharding.Mesh(
        mesh.devices.reshape(rows_count // 32, 4, 4, 2, cols_count), ROWS + ("cols",)
    )
    return jax.shard_map(
        per_device,
        mesh=split,
        in_specs=(
            P("cols", ROWS),
            P(),
            P(),
            P(ROWS, None, None, None),
            P(ROWS, None),
            P(ROWS),
            P("cols", ROWS),
        ),
        out_specs=(P("cols", ROWS), P("cols", ROWS), P("cols", None), P("cols")),
        check_vma=False,
    )
```
